256 devices in a mesh: req: 32 (over z, x_lo, core), tp: 8 (over x_hi, y).
Axes of the slice: x: 4 (x_hi: 2, x_lo: 2; x = x_hi * 2 + x_lo), y: 4, z: 8, core: 2. Of those that a mesh axis runs over, the one named last changes fastest.
Arguments:
- queries: bfloat16 [12288, 8192], P('req', 'tp'), may hold values from -40 to 40
- suffix_kv: bfloat16 [2, 12288, 1024], P(None, 'req', 'tp'), may hold values from -4 to 4
- prefix_kv: bfloat16 [2, 32, 256, 1024], P(None, 'req', 'tp'), may hold values from -4 to 4
- suffix_length: int32 [31], replicated, may hold values from 16 to 384, as said below
- request_group: int32 [31], replicated, may hold values from 0 to 3
- request_order: int32 [31], replicated, may hold values from 0 to 30, each once
- owner_map: int32 [32], replicated, may hold values from 0 to 31, each once
Outputs:
- attention: bfloat16 [12288, 8192], P('req', 'tp')
The draws below stay inside these ranges and needn't reach their ends.
Inputs may be any that keep to these rules, and one draw needn't show every extreme that they name: `suffix_length`: every suffix has 16 to 384 tokens; in every draw one suffix has exactly 384 tokens and one exactly 16.
All inputs are finite; a program needn't handle non-finite values.
Results may differ from the reference program's by a relative error of at most 0.007.
Values may be sent and summed in bfloat16 or wider, within the bound.
No kernel may reach another device: no remote copies, remote signals or barrier semaphores. Data moves between devices by JAX's collectives and lax.ppermute only.
A program may use at most 128 MiB of HBM per device.

```python
import math
import jax
import jax.numpy as jnp
from jax import lax

QH = 64
KVH = 8
HD = 128
GROUPS = 4
MINLEN = 16
MAXLEN = 384
TOK_DEV = 384
PBLK = 256
REQS = 31
SLOTS = 12288
N_REQ = 32


def shared_rows(key):
    kv_key = jax.random.fold_in(key, 101)
    query_key = jax.random.fold_in(key, 202)
    kv_rows = jnp.clip(jax.random.normal(kv_key, (2, SLOTS, KVH * HD), jnp.float32), -4.0, 4.0)
    query_rows = jnp.clip(jax.random.normal(query_key, (SLOTS, QH * HD), jnp.float32), -4.0, 4.0)
    return (kv_rows, query_rows)


def draw_queries(key, part):
    return shared_rows(key)[1].astype(jnp.bfloat16)


def draw_suffix_kv(key, part):
    return shared_rows(key)[0].astype(jnp.bfloat16)


def draw_suffix_length(key, part):
    lengths = jax.random.randint(jax.random.fold_in(key, 7), (REQS,), MINLEN, MAXLEN + 1)
    longest = jax.random.randint(jax.random.fold_in(key, 8), (), 0, REQS)
    lengths = lengths.at[longest].set(MAXLEN)
    lengths = lengths.at[(longest + 1) % REQS].set(MINLEN)
    return lengths.astype(jnp.int32)


def place_ends(drawn, rng, smallest, top_value):
    dims = drawn.shape
    spot = [jax.random.randint(jax.random.fold_in(rng, axis), (), 0, dims[axis]) for axis in range(len(dims))]
    drawn = drawn.at[tuple(spot)].set(smallest)
    longest = dims.index(max(dims))
    spot[longest] = (spot[longest] + 1) % dims[longest]
    return drawn.at[tuple(spot)].set(top_value)


def block_levels(own_key, extent, split, smallest, high):
    level = 1.0
    for dim, parts in split:
        steps = jax.random.uniform(jax.random.fold_in(jax.random.fold_in(own_key, 6), dim), (parts,), jnp.float32, smallest / len(split), high / len(split))
        level = level * jnp.repeat(jnp.exp(steps), extent[dim] // parts).reshape((-1,) + (1,) * (len(extent) - 1 - dim))
    return level


def scatter_about(own_key, extent, scale, most, shards=(), kind=jnp.bfloat16):
    gain = block_levels(own_key, extent, shards, -0.22, 0.18) if shards else 1.0
    entries = jax.random.normal(own_key, extent, jnp.float32) * scale * gain
    return jnp.minimum(jnp.maximum(entries, -most), most).astype(kind)


def setup_inputs(seed: int = 0) -> dict:
    key_of = jax.random.split(jax.random.key(seed), 8)
    queries = draw_queries(jax.random.fold_in(key_of[7], 71), 0)
    suffix_kv = draw_suffix_kv(jax.random.fold_in(key_of[7], 71), 0)
    prefix_kv = scatter_about(key_of[2], (2, N_REQ, PBLK, KVH * HD), 1.0, 4.0, ((1, 32), (2, 8)))
    suffix_length = draw_suffix_length(jax.random.fold_in(key_of[7], 71), 0)
    request_group = place_ends(jax.random.randint(key_of[4], (REQS,), 0, GROUPS), jax.random.fold_in(key_of[4], 1), 0, GROUPS - 1).astype(jnp.int32)
    request_order = jax.random.permutation(key_of[5], REQS).astype(jnp.int32)
    owner_map = jax.random.permutation(key_of[6], N_REQ).astype(jnp.int32)
    return {"queries": queries, "suffix_kv": suffix_kv, "prefix_kv": prefix_kv, "suffix_length": suffix_length, "request_group": request_group, "request_order": request_order, "owner_map": owner_map}


masked_score = -1e+30

def pack_index(slot_ids, starts, stops):
    inside = (starts[None, :] <= slot_ids[:, None]) & (slot_ids[:, None] < stops[None, :])
    request_ids = jnp.arange(starts.shape[0], dtype=jnp.int32)
    found = lax.optimization_barrier(jnp.sum(jnp.where(inside, request_ids[None, :], 0), axis=1)).astype(jnp.int32)
    missing = jnp.where(jnp.any(inside, axis=1), 0, starts.shape[0]).astype(jnp.int32)
    return (found + missing).astype(jnp.int32)

def reference(queries, suffix_kv, prefix_kv, suffix_length, request_group, request_order, owner_map):
    per_kv = QH // KVH
    score_scale = 1.0 / math.sqrt(HD)
    packed_length = jnp.take(suffix_length, request_order).astype(jnp.int32)
    packed_group = jnp.take(request_group, request_order).astype(jnp.int32)
    starts = ((jnp.arange(REQS, dtype=jnp.int32) + 1) * TOK_DEV - packed_length // 2).astype(jnp.int32)
    stops = (starts + packed_length).astype(jnp.int32)
    block_ids = jnp.arange(N_REQ, dtype=jnp.int32)
    stored_group = lax.optimization_barrier(jnp.sum(jnp.where(owner_map[None, :] == block_ids[:, None], (block_ids // (N_REQ // GROUPS))[None, :], 0), axis=1)).astype(jnp.int32)
    key_group = jnp.repeat(stored_group, PBLK)
    prefix_keys = prefix_kv[0].reshape(N_REQ * PBLK, KVH, HD).astype(jnp.float32)
    prefix_values = prefix_kv[1].reshape(N_REQ * PBLK, KVH, HD).astype(jnp.float32)
    padded = jnp.concatenate([jnp.zeros((2, TOK_DEV, KVH * HD), suffix_kv.dtype), suffix_kv], axis=1)

    def one_device(device):
        first_slot = (device * TOK_DEV).astype(jnp.int32)
        slot_ids = first_slot + jnp.arange(TOK_DEV, dtype=jnp.int32)
        own_pack = pack_index(slot_ids, starts, stops)
        is_live = own_pack < REQS
        slot_group = jnp.take(packed_group, jnp.minimum(own_pack, REQS - 1))
        near_slots = first_slot - TOK_DEV + jnp.arange(2 * TOK_DEV, dtype=jnp.int32)
        near_pack = pack_index(near_slots, starts, stops)
        nearby = lax.dynamic_slice_in_dim(padded, first_slot, 2 * TOK_DEV, 1)
        suffix_visible = (near_pack[None, :] == own_pack[:, None]) & (near_slots[None, :] <= slot_ids[:, None]) & (near_slots[None, :] >= 0)
        prefix_visible = key_group[None, :] == slot_group[:, None]
        visible = jnp.concatenate([prefix_visible, suffix_visible], axis=1) & is_live[:, None]
        query_rows = lax.dynamic_slice_in_dim(queries, first_slot, TOK_DEV, 0).reshape(TOK_DEV, KVH, per_kv, HD).astype(jnp.float32)
        near_keys = nearby[0].reshape(2 * TOK_DEV, KVH, HD).astype(jnp.float32)
        near_values = nearby[1].reshape(2 * TOK_DEV, KVH, HD).astype(jnp.float32)

        def one_head(kv_head):
            head_queries = jnp.take(query_rows, kv_head, axis=1)
            key_rows = jnp.concatenate([jnp.take(prefix_keys, kv_head, axis=1), jnp.take(near_keys, kv_head, axis=1)], axis=0)
            value_rows = jnp.concatenate([jnp.take(prefix_values, kv_head, axis=1), jnp.take(near_values, kv_head, axis=1)], axis=0)
            scores = jnp.einsum('tqd,kd->tqk', head_queries, key_rows) * score_scale
            allowed = visible[:, None, :]
            scores = jnp.where(allowed, scores, masked_score)
            row_max = lax.optimization_barrier(jnp.max(scores, axis=-1, keepdims=True))
            weights = jnp.where(allowed, jnp.exp(scores - row_max), 0.0)
            row_sum = lax.optimization_barrier(jnp.sum(weights, axis=-1))
            rounded = lax.optimization_barrier(weights.astype(jnp.bfloat16)).astype(jnp.float32)
            weighted = jnp.einsum('tqk,kd->tqd', rounded, value_rows)
            divisor = jnp.where(is_live[:, None], row_sum, 1.0)
            return jnp.where(is_live[:, None, None], weighted / divisor[..., None], 0.0)
        heads_out = lax.map(one_head, jnp.arange(KVH, dtype=jnp.int32))
        return jnp.transpose(heads_out, (1, 0, 2, 3)).reshape(TOK_DEV, QH * HD).astype(jnp.bfloat16)
    outputs = lax.map(one_device, jnp.arange(N_REQ, dtype=jnp.int32))
    return outputs.reshape(SLOTS, QH * HD)
```

```python
import functools
import math

import jax
import jax.numpy as jnp
from jax import lax
from jax.experimental import pallas as pl
from jax.experimental.pallas import tpu as pltpu
from jax.sharding import PartitionSpec as P

QH = 64
KVH = 8
HD = 128
GROUPS = 4

masked_score = -1e30
TILE = 64
CHUNK = 512


def from_behind(block, axis, distance):
    devices = range(lax.axis_size(axis))
    route = [(i - distance, i) for i in devices if i - distance in devices]
    return lax.ppermute(block, axis, route)


def attend_kernel(
    scal_ref, q_ref, pk_ref, pv_ref, s0_ref, s1_ref, o_ref, *, per_kv, tiles_per_half, half
):
    h = pl.program_id(0)
    i = pl.program_id(1)
    base = scal_ref[0]
    start = jnp.where(h == 0, scal_ref[1], scal_ref[3])
    stop = jnp.where(h == 0, scal_ref[2], scal_ref[4])
    slot0 = base + h * half + i * TILE
    any_live = (start < slot0 + TILE) & (stop > slot0)
    rows = per_kv * TILE
    scale = 1.0 / math.sqrt(HD)

    @pl.when(jnp.logical_not(any_live))
    def _():
        o_ref[...] = jnp.zeros_like(o_ref)

    def body(s_ref, key_base, n_suffix):
        q = jnp.concatenate([q_ref[:, j * HD : (j + 1) * HD] for j in range(per_kv)], axis=0)
        row = lax.broadcasted_iota(jnp.int32, (rows, 1), 0)
        slot = slot0 + jnp.bitwise_and(row, TILE - 1)
        live = (slot >= start) & (slot < stop)
        key_slot = key_base + lax.broadcasted_iota(jnp.int32, (1, n_suffix), 1)
        suffix_ok = (key_slot >= start) & (key_slot <= slot) & live

        def scores(k):
            return (
                lax.dot_general(
                    q, k, (((1,), (1,)), ((), ())), preferred_element_type=jnp.float32
                )
                * scale
            )

        n_chunks = pk_ref.shape[0] // CHUNK

        def max_step(c, m):
            k = pk_ref[pl.ds(pl.multiple_of(c * CHUNK, CHUNK), CHUNK), :]
            s = jnp.where(live, scores(k), masked_score)
            return jnp.maximum(m, jnp.max(s, axis=1, keepdims=True))

        m = jnp.full((rows, 1), masked_score, jnp.float32)
        m = lax.fori_loop(0, n_chunks, max_step, m)
        s_suf = jnp.where(suffix_ok, scores(s_ref[0]), masked_score)
        m = jnp.maximum(m, jnp.max(s_suf, axis=1, keepdims=True))

        def sum_step(c, carry):
            l, acc = carry
            at = pl.ds(pl.multiple_of(c * CHUNK, CHUNK), CHUNK)
            s = scores(pk_ref[at, :])
            p = jnp.where(live, jnp.exp(s - m), 0.0)
            l = l + jnp.sum(p, axis=1, keepdims=True)
            acc = acc + jnp.dot(
                p.astype(jnp.bfloat16), pv_ref[at, :], preferred_element_type=jnp.float32
            )
            return (l, acc)

        l = jnp.zeros((rows, 1), jnp.float32)
        acc = jnp.zeros((rows, HD), jnp.float32)
        l, acc = lax.fori_loop(0, n_chunks, sum_step, (l, acc))
        p = jnp.where(suffix_ok, jnp.exp(s_suf - m), 0.0)
        l = l + jnp.sum(p, axis=1, keepdims=True)
        acc = acc + jnp.dot(p.astype(jnp.bfloat16), s_ref[1], preferred_element_type=jnp.float32)
        out = jnp.where(live, acc / jnp.where(live, l, 1.0), 0.0).astype(o_ref.dtype)
        for j in range(per_kv):
            o_ref[:, j * HD : (j + 1) * HD] = out[j * TILE : (j + 1) * TILE, :]

    @pl.when(any_live & (h == 0))
    def _():
        body(s0_ref, base - half, s0_ref.shape[1])

    @pl.when(any_live & (h == 1))
    def _():
        body(s1_ref, base + half, s1_ref.shape[1])


def per_device(
    queries, suffix_kv, prefix_kv, suffix_length, request_group, request_order, owner_map
):
    tok_rows = queries.shape[0]
    head_cols = suffix_kv.shape[2]
    kv_heads = head_cols // HD
    per_kv = queries.shape[1] // head_cols
    stored_count = owner_map.shape[0]
    per_group = stored_count // GROUPS
    requests = suffix_length.shape[0]
    half = tok_rows // 2
    packed_length = jnp.take(suffix_length, request_order)
    packed_group = jnp.take(request_group, request_order)
    starts = (jnp.arange(requests, dtype=jnp.int32) + 1) * tok_rows - packed_length // 2
    stops = starts + packed_length
    device = lax.axis_index("req")
    base = device * tok_rows
    first = jnp.clip(device - 1, 0, requests - 1)
    second = jnp.clip(device, 0, requests - 1)
    has_first = device >= 1
    has_second = device < requests
    start0 = jnp.where(has_first, starts[first], -1)
    stop0 = jnp.where(has_first, stops[first], -1)
    start1 = jnp.where(has_second, starts[second], -1)
    stop1 = jnp.where(has_second, stops[second], -1)
    scal = jnp.stack([base, start0, stop0, start1, stop1, base, base, base]).astype(jnp.int32)
    groups = jnp.stack([packed_group[first], packed_group[second]])
    rows_of = jnp.take(
        owner_map, groups[:, None] * per_group + jnp.arange(per_group, dtype=jnp.int32)[None, :]
    )

    local = lax.all_to_all(prefix_kv, "tp", split_axis=3, concat_axis=2, tiled=True)
    stored = lax.all_gather(local, "req", axis=1, tiled=True)
    block_rows = stored.shape[2]
    picked = jnp.take(stored, rows_of.reshape(-1), axis=1)
    picked = picked.reshape(2, 2, per_group * block_rows, HD)
    pk = picked[0]
    pv = picked[1]

    earlier = from_behind(suffix_kv[:, half:, :], "req", 1)
    s0 = jnp.concatenate([earlier, suffix_kv[:, :half, :]], axis=1)
    pad = (-half) % 128
    s1 = jnp.concatenate(
        [suffix_kv[:, half:, :], jnp.zeros((2, pad, head_cols), suffix_kv.dtype)], axis=1
    )

    tiles_per_half = half // TILE
    grid = (2, tiles_per_half)
    kernel = functools.partial(
        attend_kernel, per_kv=per_kv, tiles_per_half=tiles_per_half, half=half
    )
    prefix_rows = per_group * block_rows
    return pl.pallas_call(
        kernel,
        out_shape=jax.ShapeDtypeStruct((tok_rows, per_kv * HD), queries.dtype),
        grid_spec=pltpu.PrefetchScalarGridSpec(
            num_scalar_prefetch=1,
            grid=grid,
            in_specs=[
                pl.BlockSpec((TILE, per_kv * HD), lambda h, i, s: (h * tiles_per_half + i, 0)),
                pl.BlockSpec((None, prefix_rows, HD), lambda h, i, s: (h, 0, 0)),
                pl.BlockSpec((None, prefix_rows, HD), lambda h, i, s: (h, 0, 0)),
                pl.BlockSpec(s0.shape, lambda h, i, s: (0, 0, 0)),
                pl.BlockSpec(s1.shape, lambda h, i, s: (0, 0, 0)),
            ],
            out_specs=pl.BlockSpec((TILE, per_kv * HD), lambda h, i, s: (h * tiles_per_half + i, 0)),
        ),
        compiler_params=pltpu.CompilerParams(dimension_semantics=("arbitrary", "arbitrary")),
    )(scal, queries, pk, pv, s0, s1)


def solution(mesh):
    in_specs = (
        P("req", "tp"),
        P(None, "req", "tp"),
        P(None, "req", "tp", None),
        P(),
        P(),
        P(),
        P(),
    )
    out_specs = P("req", "tp")
    return jax.shard_map(
        per_device, mesh=mesh, in_specs=in_specs, out_specs=out_specs, check_vma=False
    )
```

```python
import functools
import math

import jax
import jax.numpy as jnp
from jax import lax
from jax.experimental import pallas as pl
from jax.experimental.pallas import tpu as pltpu
from jax.sharding import PartitionSpec as P

QH = 64
KVH = 8
HD = 128
GROUPS = 4

masked_score = -1e30
TILE = 64
CHUNK = 512


def from_behind(block, axis, distance):
    devices = range(lax.axis_size(axis))
    route = [(i - distance, i) for i in devices if i - distance in devices]
    return lax.ppermute(block, axis, route)


def attend_kernel(
    scal_ref, q_ref, pk_ref, pv_ref, s0_ref, s1_ref, o_ref, *, per_kv, tiles_per_half, half
):
    h = pl.program_id(0)
    i = pl.program_id(1)
    base = scal_ref[0]
    start = jnp.where(h == 0, scal_ref[1], scal_ref[3])
    stop = jnp.where(h == 0, scal_ref[2], scal_ref[4])
    slot0 = base + h * half + i * TILE
    any_live = (start < slot0 + TILE) & (stop > slot0)
    rows = per_kv * TILE
    scale = 1.0 / math.sqrt(HD)

    @pl.when(jnp.logical_not(any_live))
    def _():
        o_ref[...] = jnp.zeros_like(o_ref)

    def body(s_ref, key_base, n_suffix):
        q = jnp.concatenate([q_ref[:, j * HD : (j + 1) * HD] for j in range(per_kv)], axis=0)
        row = lax.broadcasted_iota(jnp.int32, (rows, 1), 0)
        slot = slot0 + jnp.bitwise_and(row, TILE - 1)
        live = (slot >= start) & (slot < stop)
        key_slot = key_base + lax.broadcasted_iota(jnp.int32, (1, n_suffix), 1)
        suffix_ok = (key_slot >= start) & (key_slot <= slot) & live

        def scores(k):
            return (
                lax.dot_general(
                    q, k, (((1,), (1,)), ((), ())), preferred_element_type=jnp.float32
                )
                * scale
            )

        n_chunks = pk_ref.shape[0] // CHUNK

        def max_step(c, m):
            k = pk_ref[pl.ds(pl.multiple_of(c * CHUNK, CHUNK), CHUNK), :]
            s = jnp.where(live, scores(k), masked_score)
            return jnp.maximum(m, jnp.max(s, axis=1, keepdims=True))

        m = jnp.full((rows, 1), masked_score, jnp.float32)
        m = lax.fori_loop(0, n_chunks, max_step, m)
        s_suf = jnp.where(suffix_ok, scores(s_ref[0]), masked_score)
        m = jnp.maximum(m, jnp.max(s_suf, axis=1, keepdims=True))

        def sum_step(c, carry):
            l, acc = carry
            at = pl.ds(pl.multiple_of(c * CHUNK, CHUNK), CHUNK)
            s = scores(pk_ref[at, :])
            p = jnp.where(live, jnp.exp(s - m), 0.0)
            l = l + jnp.sum(p, axis=1, keepdims=True)
            acc = acc + jnp.dot(
                p.astype(jnp.bfloat16), pv_ref[at, :], preferred_element_type=jnp.float32
            )
            return (l, acc)

        l = jnp.zeros((rows, 1), jnp.float32)
        acc = jnp.zeros((rows, HD), jnp.float32)
        l, acc = lax.fori_loop(0, n_chunks, sum_step, (l, acc))
        p = jnp.where(suffix_ok, jnp.exp(s_suf - m), 0.0)
        l = l + jnp.sum(p, axis=1, keepdims=True)
        acc = acc + jnp.dot(p.astype(jnp.bfloat16), s_ref[1], preferred_element_type=jnp.float32)
        out = jnp.where(live, acc / jnp.where(live, l, 1.0), 0.0).astype(o_ref.dtype)
        for j in range(per_kv):
            o_ref[:, j * HD : (j + 1) * HD] = out[j * TILE : (j + 1) * TILE, :]

    @pl.when(any_live & (h == 0))
    def _():
        body(s0_ref, base - half, s0_ref.shape[1])

    @pl.when(any_live & (h == 1))
    def _():
        body(s1_ref, base + half, s1_ref.shape[1])


def per_device(
    queries, suffix_kv, prefix_kv, suffix_length, request_group, request_order, owner_map
):
    tok_rows = queries.shape[0]
    head_cols = suffix_kv.shape[2]
    kv_heads = head_cols // HD
    per_kv = queries.shape[1] // head_cols
    stored_count = owner_map.shape[0]
    per_group = stored_count // GROUPS
    requests = suffix_length.shape[0]
    half = tok_rows // 2
    packed_length = jnp.take(suffix_length, request_order)
    packed_group = jnp.take(request_group, request_order)
    starts = (jnp.arange(requests, dtype=jnp.int32) + 1) * tok_rows - packed_length // 2
    stops = starts + packed_length
    device = lax.axis_index(("chip", "core"))
    base = device * tok_rows
    first = jnp.clip(device - 1, 0, requests - 1)
    second = jnp.clip(device, 0, requests - 1)
    has_first = device >= 1
    has_second = device < requests
    start0 = jnp.where(has_first, starts[first], -1)
    stop0 = jnp.where(has_first, stops[first], -1)
    start1 = jnp.where(has_second, starts[second], -1)
    stop1 = jnp.where(has_second, stops[second], -1)
    scal = jnp.stack([base, start0, stop0, start1, stop1, base, base, base]).astype(jnp.int32)
    groups = jnp.stack([packed_group[first], packed_group[second]])
    rows_of = jnp.take(
        owner_map, groups[:, None] * per_group + jnp.arange(per_group, dtype=jnp.int32)[None, :]
    )

    tp = lax.axis_index("tp")
    n_tp = lax.axis_size("tp")
    pieces = []
    for k in range(n_tp):
        col = ((tp + k) % n_tp) * HD
        piece = lax.dynamic_slice_in_dim(prefix_kv, col, HD, axis=3)
        if k:
            piece = lax.ppermute(piece, "tp", [(j, (j + k) % n_tp) for j in range(n_tp)])
        pieces.append(piece)
    local = jnp.concatenate(pieces, axis=2)
    own = lax.all_gather(local, "chip", axis=1, tiled=True)
    other = lax.ppermute(own, "core", [(0, 1), (1, 0)])
    stored = jnp.concatenate([own, other], axis=1)
    per_chip = own.shape[1]
    block_rows = stored.shape[2]
    core = lax.axis_index("core")
    flat = rows_of.reshape(-1)
    where_stored = jnp.where(flat % 2 == core, 0, per_chip) + flat // 2
    picked = jnp.take(stored, where_stored, axis=1)
    picked = picked.reshape(2, 2, per_group * block_rows, HD)
    pk = picked[0]
    pv = picked[1]

    earlier = from_behind(suffix_kv[:, half:, :], ("chip", "core"), 1)
    s0 = jnp.concatenate([earlier, suffix_kv[:, :half, :]], axis=1)
    pad = (-half) % 128
    s1 = jnp.concatenate(
        [suffix_kv[:, half:, :], jnp.zeros((2, pad, head_cols), suffix_kv.dtype)], axis=1
    )

    tiles_per_half = half // TILE
    grid = (2, tiles_per_half)
    kernel = functools.partial(
        attend_kernel, per_kv=per_kv, tiles_per_half=tiles_per_half, half=half
    )
    prefix_rows = per_group * block_rows
    return pl.pallas_call(
        kernel,
        out_shape=jax.ShapeDtypeStruct((tok_rows, per_kv * HD), queries.dtype),
        grid_spec=pltpu.PrefetchScalarGridSpec(
            num_scalar_prefetch=1,
            grid=grid,
            in_specs=[
                pl.BlockSpec((TILE, per_kv * HD), lambda h, i, s: (h * tiles_per_half + i, 0)),
                pl.BlockSpec((None, prefix_rows, HD), lambda h, i, s: (h, 0, 0)),
                pl.BlockSpec((None, prefix_rows, HD), lambda h, i, s: (h, 0, 0)),
                pl.BlockSpec(s0.shape, lambda h, i, s: (0, 0, 0)),
                pl.BlockSpec(s1.shape, lambda h, i, s: (0, 0, 0)),
            ],
            out_specs=pl.BlockSpec((TILE, per_kv * HD), lambda h, i, s: (h * tiles_per_half + i, 0)),
        ),
        compiler_params=pltpu.CompilerParams(dimension_semantics=("arbitrary", "arbitrary")),
    )(scal, queries, pk, pv, s0, s1)


def solution(mesh):
    devices = mesh.devices
    n_req, n_tp = devices.shape
    split = jax.sharding.Mesh(devices.reshape(n_req // 2, 2, n_tp), ("chip", "core", "tp"))
    req = ("chip", "core")
    in_specs = (
        P(req, "tp"),
        P(None, req, "tp"),
        P(None, req, "tp", None),
        P(),
        P(),
        P(),
        P(),
    )
    out_specs = P(req, "tp")
    return jax.shard_map(
        per_device, mesh=split, in_specs=in_specs, out_specs=out_specs, check_vma=False
    )
```

```python
import functools
import math

import jax
import jax.numpy as jnp
from jax import lax
from jax.experimental import pallas as pl
from jax.experimental.pallas import tpu as pltpu
from jax.sharding import PartitionSpec as P

QH = 64
KVH = 8
HD = 128
GROUPS = 4

masked_score = -1e30
TILE = 64
CHUNK = 512


def from_behind(block, axis, distance):
    devices = range(lax.axis_size(axis))
    route = [(i - distance, i) for i in devices if i - distance in devices]
    return lax.ppermute(block, axis, route)


def attend_kernel(
    scal_ref, q_ref, stored_ref, s0_ref, s1_ref, o_ref, buf, sems, *, per_kv, half, n_blocks
):
    h = pl.program_id(0)
    i = pl.program_id(1)
    base = scal_ref[0]
    start = jnp.where(h == 0, scal_ref[1], scal_ref[3])
    stop = jnp.where(h == 0, scal_ref[2], scal_ref[4])
    slot0 = base + h * half + i * TILE
    any_live = (start < slot0 + TILE) & (stop > slot0)
    rows = per_kv * TILE
    scale = 1.0 / math.sqrt(HD)
    block_rows = stored_ref.shape[2]

    def block_copy(hh, b):
        src = stored_ref.at[:, scal_ref[8 + hh * n_blocks + b]]
        dst = buf.at[hh, :, pl.ds(b * block_rows, block_rows), :]
        return pltpu.make_async_copy(src, dst, sems.at[hh, b])

    @pl.when((h == 0) & (i == 0))
    def _():
        for hh in range(2):
            for b in range(n_blocks):
                block_copy(hh, b).start()

    @pl.when(jnp.logical_not(any_live))
    def _():
        o_ref[...] = jnp.zeros_like(o_ref)

    def body(hh, s_ref, key_base, n_suffix):
        @pl.when(i == 0)
        def _():
            for b in range(n_blocks):
                block_copy(hh, b).wait()

        @pl.when(any_live)
        def _():
            compute(hh, s_ref, key_base, n_suffix)

    def compute(hh, s_ref, key_base, n_suffix):
        kref = buf.at[hh, 0]
        vref = buf.at[hh, 1]
        q = jnp.concatenate([q_ref[:, j * HD : (j + 1) * HD] for j in range(per_kv)], axis=0)
        row = lax.broadcasted_iota(jnp.int32, (rows, 1), 0)
        slot = slot0 + jnp.bitwise_and(row, TILE - 1)
        live = (slot >= start) & (slot < stop)
        key_slot = key_base + lax.broadcasted_iota(jnp.int32, (1, n_suffix), 1)
        suffix_ok = (key_slot >= start) & (key_slot <= slot) & live

        def raw(k):
            return lax.dot_general(
                q, k, (((1,), (1,)), ((), ())), preferred_element_type=jnp.float32
            )

        n_chunks = kref.shape[0] // CHUNK

        def max_step(c, m):
            s = raw(kref[pl.ds(pl.multiple_of(c * CHUNK, CHUNK), CHUNK), :])
            return jnp.maximum(m, jnp.max(s, axis=1, keepdims=True))

        m = jnp.full((rows, 1), masked_score, jnp.float32)
        m = lax.fori_loop(0, n_chunks, max_step, m)
        s_suf = raw(s_ref[0]) * scale
        m = jnp.maximum(m * scale, jnp.max(jnp.where(suffix_ok, s_suf, masked_score), axis=1, keepdims=True))

        def sum_step(c, carry):
            l, acc = carry
            at = pl.ds(pl.multiple_of(c * CHUNK, CHUNK), CHUNK)
            p = jnp.exp(raw(kref[at, :]) * scale - m)
            l = l + jnp.sum(p, axis=1, keepdims=True)
            acc = acc + jnp.dot(
                p.astype(jnp.bfloat16), vref[at, :], preferred_element_type=jnp.float32
            )
            return (l, acc)

        l = jnp.zeros((rows, 1), jnp.float32)
        acc = jnp.zeros((rows, HD), jnp.float32)
        l, acc = lax.fori_loop(0, n_chunks, sum_step, (l, acc))
        p = jnp.where(suffix_ok, jnp.exp(s_suf - m), 0.0)
        l = l + jnp.sum(p, axis=1, keepdims=True)
        acc = acc + jnp.dot(p.astype(jnp.bfloat16), s_ref[1], preferred_element_type=jnp.float32)
        out = jnp.where(live, acc / jnp.where(live, l, 1.0), 0.0).astype(o_ref.dtype)
        for j in range(per_kv):
            o_ref[:, j * HD : (j + 1) * HD] = out[j * TILE : (j + 1) * TILE, :]

    @pl.when(h == 0)
    def _():
        body(0, s0_ref, base - half, s0_ref.shape[1])

    @pl.when(h == 1)
    def _():
        body(1, s1_ref, base + half, s1_ref.shape[1])


def per_device(
    queries, suffix_kv, prefix_kv, suffix_length, request_group, request_order, owner_map
):
    tok_rows = queries.shape[0]
    head_cols = suffix_kv.shape[2]
    kv_heads = head_cols // HD
    per_kv = queries.shape[1] // head_cols
    stored_count = owner_map.shape[0]
    per_group = stored_count // GROUPS
    requests = suffix_length.shape[0]
    half = tok_rows // 2
    packed_length = jnp.take(suffix_length, request_order)
    packed_group = jnp.take(request_group, request_order)
    starts = (jnp.arange(requests, dtype=jnp.int32) + 1) * tok_rows - packed_length // 2
    stops = starts + packed_length
    device = lax.axis_index("req")
    base = device * tok_rows
    first = jnp.clip(device - 1, 0, requests - 1)
    second = jnp.clip(device, 0, requests - 1)
    has_first = device >= 1
    has_second = device < requests
    start0 = jnp.where(has_first, starts[first], -1)
    stop0 = jnp.where(has_first, stops[first], -1)
    start1 = jnp.where(has_second, starts[second], -1)
    stop1 = jnp.where(has_second, stops[second], -1)
    groups = jnp.stack([packed_group[first], packed_group[second]])
    rows_of = jnp.take(
        owner_map, groups[:, None] * per_group + jnp.arange(per_group, dtype=jnp.int32)[None, :]
    )
    head = jnp.stack([base, start0, stop0, start1, stop1, base, base, base])
    scal = jnp.concatenate([head, rows_of.reshape(-1)]).astype(jnp.int32)

    local = lax.all_to_all(prefix_kv, "tp", split_axis=3, concat_axis=2, tiled=True)
    stored = lax.all_gather(local, "req", axis=1, tiled=True)
    earlier = from_behind(suffix_kv[:, half:, :], "req", 1)
    s0 = jnp.concatenate([earlier, suffix_kv[:, :half, :]], axis=1)
    pad = (-half) % 128
    s1 = jnp.concatenate(
        [suffix_kv[:, half:, :], jnp.zeros((2, pad, head_cols), suffix_kv.dtype)], axis=1
    )

    tiles_per_half = half // TILE
    grid = (2, tiles_per_half)
    kernel = functools.partial(attend_kernel, per_kv=per_kv, half=half, n_blocks=per_group)
    block_rows = stored.shape[2]
    prefix_rows = per_group * block_rows
    tile_map = lambda h, i, s: (h * tiles_per_half + i, 0)
    return pl.pallas_call(
        kernel,
        out_shape=jax.ShapeDtypeStruct((tok_rows, per_kv * HD), queries.dtype),
        grid_spec=pltpu.PrefetchScalarGridSpec(
            num_scalar_prefetch=1,
            grid=grid,
            in_specs=[
                pl.BlockSpec((TILE, per_kv * HD), tile_map),
                pl.BlockSpec(memory_space=pl.ANY),
                pl.BlockSpec(s0.shape, lambda h, i, s: (0, 0, 0)),
                pl.BlockSpec(s1.shape, lambda h, i, s: (0, 0, 0)),
            ],
            out_specs=pl.BlockSpec((TILE, per_kv * HD), tile_map),
            scratch_shapes=[
                pltpu.VMEM((2, 2, prefix_rows, HD), stored.dtype),
                pltpu.SemaphoreType.DMA((2, per_group)),
            ],
        ),
        compiler_params=pltpu.CompilerParams(dimension_semantics=("arbitrary", "arbitrary")),
    )(scal, queries, stored, s0, s1)


def solution(mesh):
    in_specs = (
        P("req", "tp"),
        P(None, "req", "tp"),
        P(None, "req", "tp", None),
        P(),
        P(),
        P(),
        P(),
    )
    out_specs = P("req", "tp")
    return jax.shard_map(
        per_device, mesh=mesh, in_specs=in_specs, out_specs=out_specs, check_vma=False
    )
```

```python
import functools
import math

import jax
import jax.numpy as jnp
from jax import lax
from jax.experimental import pallas as pl
from jax.experimental.pallas import tpu as pltpu
from jax.sharding import PartitionSpec as P

QH = 64
KVH = 8
HD = 128
GROUPS = 4

masked_score = -1e30
TILE = 64
CHUNK = 512


def from_behind(block, axis, distance):
    devices = range(lax.axis_size(axis))
    route = [(i - distance, i) for i in devices if i - distance in devices]
    return lax.ppermute(block, axis, route)


def ring_gather(block, wanted):
    n = lax.axis_size("req")
    r = lax.axis_index("req")
    core = r % 2
    pair = (r // 2) % 2
    n_z = n // 4
    reach = n_z // 2

    def route(fn):
        return [(i, fn(i) % n) for i in range(n)]

    other = lax.ppermute(block, "req", route(lambda i: i ^ 1))
    two = jnp.where(core == 0, jnp.concatenate([block, other], 1), jnp.concatenate([other, block], 1))
    other = lax.ppermute(two, "req", route(lambda i: i ^ 2))
    four = jnp.where(pair == 0, jnp.concatenate([two, other], 1), jnp.concatenate([other, two], 1))
    walked = [four]
    for _ in range(reach):
        walked.append(
            lax.ppermute(walked[-1], "req", route(lambda i: i + 4 if i % 2 == 0 else i - 4))
        )
    swapped = lax.ppermute(jnp.concatenate(walked[1:reach], 1), "req", route(lambda i: i ^ 1))
    stored = jnp.concatenate(walked + [swapped], 1)
    z = r // 4
    o = (wanted // 4 - z) % n_z
    p0 = jnp.where(o == 0, 0, jnp.where(o >= reach, n_z - o, reach + o))
    p1 = jnp.where(o <= reach, o, reach + n_z - o)
    return stored, jnp.where(core == 0, p0, p1) * 4 + wanted % 4


def attend_kernel(
    scal_ref, q_ref, stored_ref, s0_ref, s1_ref, o_ref, buf, sems, *, per_kv, half, n_blocks
):
    h = pl.program_id(0)
    i = pl.program_id(1)
    base = scal_ref[0]
    start = jnp.where(h == 0, scal_ref[1], scal_ref[3])
    stop = jnp.where(h == 0, scal_ref[2], scal_ref[4])
    slot0 = base + h * half + i * TILE
    any_live = (start < slot0 + TILE) & (stop > slot0)
    rows = per_kv * TILE
    scale = 1.0 / math.sqrt(HD)
    block_rows = stored_ref.shape[2]

    def block_copy(hh, b):
        src = stored_ref.at[:, scal_ref[8 + hh * n_blocks + b]]
        dst = buf.at[hh, :, pl.ds(b * block_rows, block_rows), :]
        return pltpu.make_async_copy(src, dst, sems.at[hh, b])

    @pl.when((h == 0) & (i == 0))
    def _():
        for hh in range(2):
            for b in range(n_blocks):
                block_copy(hh, b).start()

    @pl.when(jnp.logical_not(any_live))
    def _():
        o_ref[...] = jnp.zeros_like(o_ref)

    def body(hh, s_ref, key_base, n_suffix):
        @pl.when(i == 0)
        def _():
            for b in range(n_blocks):
                block_copy(hh, b).wait()

        @pl.when(any_live)
        def _():
            compute(hh, s_ref, key_base, n_suffix)

    def compute(hh, s_ref, key_base, n_suffix):
        kref = buf.at[hh, 0]
        vref = buf.at[hh, 1]
        q = jnp.concatenate([q_ref[:, j * HD : (j + 1) * HD] for j in range(per_kv)], axis=0)
        row = lax.broadcasted_iota(jnp.int32, (rows, 1), 0)
        slot = slot0 + jnp.bitwise_and(row, TILE - 1)
        live = (slot >= start) & (slot < stop)
        key_slot = key_base + lax.broadcasted_iota(jnp.int32, (1, n_suffix), 1)
        suffix_ok = (key_slot >= start) & (key_slot <= slot) & live

        def raw(k):
            return lax.dot_general(
                q, k, (((1,), (1,)), ((), ())), preferred_element_type=jnp.float32
            )

        n_chunks = kref.shape[0] // CHUNK

        def max_step(c, m):
            s = raw(kref[pl.ds(pl.multiple_of(c * CHUNK, CHUNK), CHUNK), :])
            return jnp.maximum(m, jnp.max(s, axis=1, keepdims=True))

        m = jnp.full((rows, 1), masked_score, jnp.float32)
        m = lax.fori_loop(0, n_chunks, max_step, m)
        s_suf = raw(s_ref[0]) * scale
        m = jnp.maximum(m * scale, jnp.max(jnp.where(suffix_ok, s_suf, masked_score), axis=1, keepdims=True))

        def sum_step(c, carry):
            l, acc = carry
            at = pl.ds(pl.multiple_of(c * CHUNK, CHUNK), CHUNK)
            p = jnp.exp(raw(kref[at, :]) * scale - m)
            l = l + jnp.sum(p, axis=1, keepdims=True)
            acc = acc + jnp.dot(
                p.astype(jnp.bfloat16), vref[at, :], preferred_element_type=jnp.float32
            )
            return (l, acc)

        l = jnp.zeros((rows, 1), jnp.float32)
        acc = jnp.zeros((rows, HD), jnp.float32)
        l, acc = lax.fori_loop(0, n_chunks, sum_step, (l, acc))
        p = jnp.where(suffix_ok, jnp.exp(s_suf - m), 0.0)
        l = l + jnp.sum(p, axis=1, keepdims=True)
        acc = acc + jnp.dot(p.astype(jnp.bfloat16), s_ref[1], preferred_element_type=jnp.float32)
        out = jnp.where(live, acc / jnp.where(live, l, 1.0), 0.0).astype(o_ref.dtype)
        for j in range(per_kv):
            o_ref[:, j * HD : (j + 1) * HD] = out[j * TILE : (j + 1) * TILE, :]

    @pl.when(h == 0)
    def _():
        body(0, s0_ref, base - half, s0_ref.shape[1])

    @pl.when(h == 1)
    def _():
        body(1, s1_ref, base + half, s1_ref.shape[1])


def per_device(
    queries, suffix_kv, prefix_kv, suffix_length, request_group, request_order, owner_map
):
    tok_rows = queries.shape[0]
    head_cols = suffix_kv.shape[2]
    kv_heads = head_cols // HD
    per_kv = queries.shape[1] // head_cols
    stored_count = owner_map.shape[0]
    per_group = stored_count // GROUPS
    requests = suffix_length.shape[0]
    half = tok_rows // 2
    packed_length = jnp.take(suffix_length, request_order)
    packed_group = jnp.take(request_group, request_order)
    starts = (jnp.arange(requests, dtype=jnp.int32) + 1) * tok_rows - packed_length // 2
    stops = starts + packed_length
    device = lax.axis_index("req")
    base = device * tok_rows
    first = jnp.clip(device - 1, 0, requests - 1)
    second = jnp.clip(device, 0, requests - 1)
    has_first = device >= 1
    has_second = device < requests
    start0 = jnp.where(has_first, starts[first], -1)
    stop0 = jnp.where(has_first, stops[first], -1)
    start1 = jnp.where(has_second, starts[second], -1)
    stop1 = jnp.where(has_second, stops[second], -1)
    groups = jnp.stack([packed_group[first], packed_group[second]])
    rows_of = jnp.take(
        owner_map, groups[:, None] * per_group + jnp.arange(per_group, dtype=jnp.int32)[None, :]
    )
    head = jnp.stack([base, start0, stop0, start1, stop1, base, base, base])

    local = lax.all_to_all(prefix_kv, "tp", split_axis=3, concat_axis=2, tiled=True)
    stored, where_block = ring_gather(local, rows_of.reshape(-1))
    scal = jnp.concatenate([head, where_block]).astype(jnp.int32)
    earlier = from_behind(suffix_kv[:, half:, :], "req", 1)
    s0 = jnp.concatenate([earlier, suffix_kv[:, :half, :]], axis=1)
    pad = (-half) % 128
    s1 = jnp.concatenate(
        [suffix_kv[:, half:, :], jnp.zeros((2, pad, head_cols), suffix_kv.dtype)], axis=1
    )

    tiles_per_half = half // TILE
    grid = (2, tiles_per_half)
    kernel = functools.partial(attend_kernel, per_kv=per_kv, half=half, n_blocks=per_group)
    block_rows = stored.shape[2]
    prefix_rows = per_group * block_rows
    tile_map = lambda h, i, s: (h * tiles_per_half + i, 0)
    return pl.pallas_call(
        kernel,
        out_shape=jax.ShapeDtypeStruct((tok_rows, per_kv * HD), queries.dtype),
        grid_spec=pltpu.PrefetchScalarGridSpec(
            num_scalar_prefetch=1,
            grid=grid,
            in_specs=[
                pl.BlockSpec((TILE, per_kv * HD), tile_map),
                pl.BlockSpec(memory_space=pl.ANY),
                pl.BlockSpec(s0.shape, lambda h, i, s: (0, 0, 0)),
                pl.BlockSpec(s1.shape, lambda h, i, s: (0, 0, 0)),
            ],
            out_specs=pl.BlockSpec((TILE, per_kv * HD), tile_map),
            scratch_shapes=[
                pltpu.VMEM((2, 2, prefix_rows, HD), stored.dtype),
                pltpu.SemaphoreType.DMA((2, per_group)),
            ],
        ),
        compiler_params=pltpu.CompilerParams(dimension_semantics=("arbitrary", "arbitrary")),
    )(scal, queries, stored, s0, s1)


def solution(mesh):
    in_specs = (
        P("req", "tp"),
        P(None, "req", "tp"),
        P(None, "req", "tp", None),
        P(),
        P(),
        P(),
        P(),
    )
    out_specs = P("req", "tp")
    return jax.shard_map(
        per_device, mesh=mesh, in_specs=in_specs, out_specs=out_specs, check_vma=False
    )
```

```python
import functools
import math

import jax
import jax.numpy as jnp
from jax import lax
from jax.experimental import pallas as pl
from jax.experimental.pallas import tpu as pltpu
from jax.sharding import PartitionSpec as P

QH = 64
KVH = 8
HD = 128
GROUPS = 4

masked_score = -1e30
TILE = 64
CHUNK = 512


def from_behind(block, axis, distance):
    devices = range(lax.axis_size(axis))
    route = [(i - distance, i) for i in devices if i - distance in devices]
    return lax.ppermute(block, axis, route)


def ring_gather(block, wanted):
    n = lax.axis_size("req")
    r = lax.axis_index("req")
    core = r % 2
    pair = (r // 2) % 2
    n_z = n // 4
    reach = n_z // 2

    def route(fn):
        return [(i, fn(i) % n) for i in range(n)]

    def both(x, fn):
        return [lax.ppermute(x[kv], "req", route(fn)) for kv in range(2)]

    other = lax.ppermute(block, "req", route(lambda i: i ^ 1))
    two = jnp.where(core == 0, jnp.concatenate([block, other], 1), jnp.concatenate([other, block], 1))
    two = [two[0], two[1]]
    other = both(two, lambda i: i ^ 2)
    four = [
        jnp.where(pair == 0, jnp.concatenate([t, o], 0), jnp.concatenate([o, t], 0))
        for t, o in zip(two, other)
    ]
    walked = [four]
    for _ in range(reach):
        walked.append(both(walked[-1], lambda i: i + 4 if i % 2 == 0 else i - 4))
    mine = [jnp.concatenate([w[kv] for w in walked[1:reach]], 0) for kv in range(2)]
    swapped = both(mine, lambda i: i ^ 1)
    pieces = [[w[kv] for w in walked] + [swapped[kv]] for kv in range(2)]
    z = r // 4
    o = (wanted // 4 - z) % n_z
    p0 = jnp.where(o == 0, 0, jnp.where(o >= reach, n_z - o, reach + o))
    p1 = jnp.where(o <= reach, o, reach + n_z - o)
    return pieces, jnp.where(core == 0, p0, p1) * 4 + wanted % 4


def attend_kernel(scal_ref, q_ref, *refs, per_kv, half, n_blocks, n_pieces):
    piece_refs = (refs[:n_pieces], refs[n_pieces : 2 * n_pieces])
    s0_ref, s1_ref, o_ref, buf, sems = refs[2 * n_pieces :]
    h = pl.program_id(0)
    i = pl.program_id(1)
    base = scal_ref[0]
    start = jnp.where(h == 0, scal_ref[1], scal_ref[3])
    stop = jnp.where(h == 0, scal_ref[2], scal_ref[4])
    slot0 = base + h * half + i * TILE
    any_live = (start < slot0 + TILE) & (stop > slot0)
    rows = per_kv * TILE
    scale = 1.0 / math.sqrt(HD)
    block_rows = piece_refs[0][0].shape[1]
    group = piece_refs[0][0].shape[0]
    last = n_pieces - 1

    def dst(hh, kv, b):
        return buf.at[hh, kv, pl.ds(b * block_rows, block_rows), :]

    def start_copy(hh, b):
        where = scal_ref[8 + hh * n_blocks + b]
        place = where // group
        for p in range(n_pieces):
            hit = (place == p) if p < last else (place >= last)
            at = where % group if p < last else where - last * group

            @pl.when(hit)
            def _():
                for kv in range(2):
                    pltpu.make_async_copy(
                        piece_refs[kv][p].at[at], dst(hh, kv, b), sems.at[hh, kv, b]
                    ).start()

    def wait_copy(hh, b):
        for kv in range(2):
            pltpu.make_async_copy(
                piece_refs[kv][0].at[0], dst(hh, kv, b), sems.at[hh, kv, b]
            ).wait()

    @pl.when((h == 0) & (i == 0))
    def _():
        for hh in range(2):
            for b in range(n_blocks):
                start_copy(hh, b)

    @pl.when(jnp.logical_not(any_live))
    def _():
        o_ref[...] = jnp.zeros_like(o_ref)

    def body(hh, s_ref, key_base, n_suffix):
        @pl.when(i == 0)
        def _():
            for b in range(n_blocks):
                wait_copy(hh, b)

        @pl.when(any_live)
        def _():
            compute(hh, s_ref, key_base, n_suffix)

    def compute(hh, s_ref, key_base, n_suffix):
        kref = buf.at[hh, 0]
        vref = buf.at[hh, 1]
        q = jnp.concatenate([q_ref[:, j * HD : (j + 1) * HD] for j in range(per_kv)], axis=0)
        row = lax.broadcasted_iota(jnp.int32, (rows, 1), 0)
        slot = slot0 + jnp.bitwise_and(row, TILE - 1)
        live = (slot >= start) & (slot < stop)
        key_slot = key_base + lax.broadcasted_iota(jnp.int32, (1, n_suffix), 1)
        suffix_ok = (key_slot >= start) & (key_slot <= slot) & live

        def raw(k):
            return lax.dot_general(
                q, k, (((1,), (1,)), ((), ())), preferred_element_type=jnp.float32
            )

        n_chunks = kref.shape[0] // CHUNK

        def max_step(c, m):
            s = raw(kref[pl.ds(pl.multiple_of(c * CHUNK, CHUNK), CHUNK), :])
            return jnp.maximum(m, jnp.max(s, axis=1, keepdims=True))

        m = jnp.full((rows, 1), masked_score, jnp.float32)
        m = lax.fori_loop(0, n_chunks, max_step, m)
        s_suf = raw(s_ref[0]) * scale
        m = jnp.maximum(m * scale, jnp.max(jnp.where(suffix_ok, s_suf, masked_score), axis=1, keepdims=True))

        def sum_step(c, carry):
            l, acc = carry
            at = pl.ds(pl.multiple_of(c * CHUNK, CHUNK), CHUNK)
            p = jnp.exp(raw(kref[at, :]) * scale - m)
            l = l + jnp.sum(p, axis=1, keepdims=True)
            acc = acc + jnp.dot(
                p.astype(jnp.bfloat16), vref[at, :], preferred_element_type=jnp.float32
            )
            return (l, acc)

        l = jnp.zeros((rows, 1), jnp.float32)
        acc = jnp.zeros((rows, HD), jnp.float32)
        l, acc = lax.fori_loop(0, n_chunks, sum_step, (l, acc))
        p = jnp.where(suffix_ok, jnp.exp(s_suf - m), 0.0)
        l = l + jnp.sum(p, axis=1, keepdims=True)
        acc = acc + jnp.dot(p.astype(jnp.bfloat16), s_ref[1], preferred_element_type=jnp.float32)
        out = jnp.where(live, acc / jnp.where(live, l, 1.0), 0.0).astype(o_ref.dtype)
        for j in range(per_kv):
            o_ref[:, j * HD : (j + 1) * HD] = out[j * TILE : (j + 1) * TILE, :]

    @pl.when(h == 0)
    def _():
        body(0, s0_ref, base - half, s0_ref.shape[1])

    @pl.when(h == 1)
    def _():
        body(1, s1_ref, base + half, s1_ref.shape[1])


def per_device(
    queries, suffix_kv, prefix_kv, suffix_length, request_group, request_order, owner_map
):
    tok_rows = queries.shape[0]
    head_cols = suffix_kv.shape[2]
    kv_heads = head_cols // HD
    per_kv = queries.shape[1] // head_cols
    stored_count = owner_map.shape[0]
    per_group = stored_count // GROUPS
    requests = suffix_length.shape[0]
    half = tok_rows // 2
    packed_length = jnp.take(suffix_length, request_order)
    packed_group = jnp.take(request_group, request_order)
    starts = (jnp.arange(requests, dtype=jnp.int32) + 1) * tok_rows - packed_length // 2
    stops = starts + packed_length
    device = lax.axis_index("req")
    base = device * tok_rows
    first = jnp.clip(device - 1, 0, requests - 1)
    second = jnp.clip(device, 0, requests - 1)
    has_first = device >= 1
    has_second = device < requests
    start0 = jnp.where(has_first, starts[first], -1)
    stop0 = jnp.where(has_first, stops[first], -1)
    start1 = jnp.where(has_second, starts[second], -1)
    stop1 = jnp.where(has_second, stops[second], -1)
    groups = jnp.stack([packed_group[first], packed_group[second]])
    rows_of = jnp.take(
        owner_map, groups[:, None] * per_group + jnp.arange(per_group, dtype=jnp.int32)[None, :]
    )
    head = jnp.stack([base, start0, stop0, start1, stop1, base, base, base])

    local = lax.all_to_all(prefix_kv, "tp", split_axis=3, concat_axis=2, tiled=True)
    pieces, where_block = ring_gather(local, rows_of.reshape(-1))
    scal = jnp.concatenate([head, where_block]).astype(jnp.int32)
    earlier = from_behind(suffix_kv[:, half:, :], "req", 1)
    s0 = jnp.concatenate([earlier, suffix_kv[:, :half, :]], axis=1)
    pad = (-half) % 128
    s1 = jnp.concatenate(
        [suffix_kv[:, half:, :], jnp.zeros((2, pad, head_cols), suffix_kv.dtype)], axis=1
    )

    tiles_per_half = half // TILE
    grid = (2, tiles_per_half)
    n_pieces = len(pieces[0])
    kernel = functools.partial(
        attend_kernel, per_kv=per_kv, half=half, n_blocks=per_group, n_pieces=n_pieces
    )
    block_rows = pieces[0][0].shape[1]
    prefix_rows = per_group * block_rows
    tile_map = lambda h, i, s: (h * tiles_per_half + i, 0)
    return pl.pallas_call(
        kernel,
        out_shape=jax.ShapeDtypeStruct((tok_rows, per_kv * HD), queries.dtype),
        grid_spec=pltpu.PrefetchScalarGridSpec(
            num_scalar_prefetch=1,
            grid=grid,
            in_specs=[
                pl.BlockSpec((TILE, per_kv * HD), tile_map),
                *[pl.BlockSpec(memory_space=pl.ANY)] * (2 * n_pieces),
                pl.BlockSpec(s0.shape, lambda h, i, s: (0, 0, 0)),
                pl.BlockSpec(s1.shape, lambda h, i, s: (0, 0, 0)),
            ],
            out_specs=pl.BlockSpec((TILE, per_kv * HD), tile_map),
            scratch_shapes=[
                pltpu.VMEM((2, 2, prefix_rows, HD), queries.dtype),
                pltpu.SemaphoreType.DMA((2, 2, per_group)),
            ],
        ),
        compiler_params=pltpu.CompilerParams(dimension_semantics=("arbitrary", "arbitrary")),
    )(scal, queries, *pieces[0], *pieces[1], s0, s1)


def solution(mesh):
    in_specs = (
        P("req", "tp"),
        P(None, "req", "tp"),
        P(None, "req", "tp", None),
        P(),
        P(),
        P(),
        P(),
    )
    out_specs = P("req", "tp")
    return jax.shard_map(
        per_device, mesh=mesh, in_specs=in_specs, out_specs=out_specs, check_vma=False
    )
```

```python
import functools
import math

import jax
import jax.numpy as jnp
from jax import lax
from jax.experimental import pallas as pl
from jax.experimental.pallas import tpu as pltpu
from jax.sharding import PartitionSpec as P

QH = 64
KVH = 8
HD = 128
GROUPS = 4

masked_score = -1e30
TILE = 64
CHUNK = 2048


def from_behind(block, axis, distance):
    devices = range(lax.axis_size(axis))
    route = [(i - distance, i) for i in devices if i - distance in devices]
    return lax.ppermute(block, axis, route)


def ring_gather(block, wanted):
    n = lax.axis_size("req")
    r = lax.axis_index("req")
    core = r % 2
    pair = (r // 2) % 2
    n_z = n // 4
    reach = n_z // 2

    def route(fn):
        return [(i, fn(i) % n) for i in range(n)]

    def both(x, fn):
        return [lax.ppermute(x[kv], "req", route(fn)) for kv in range(2)]

    other = lax.ppermute(block, "req", route(lambda i: i ^ 1))
    two = jnp.where(core == 0, jnp.concatenate([block, other], 1), jnp.concatenate([other, block], 1))
    two = [two[0], two[1]]
    other = both(two, lambda i: i ^ 2)
    four = [
        jnp.where(pair == 0, jnp.concatenate([t, o], 0), jnp.concatenate([o, t], 0))
        for t, o in zip(two, other)
    ]
    walked = [four]
    for _ in range(reach):
        walked.append(both(walked[-1], lambda i: i + 4 if i % 2 == 0 else i - 4))
    mine = [jnp.concatenate([w[kv] for w in walked[1:reach]], 0) for kv in range(2)]
    swapped = both(mine, lambda i: i ^ 1)
    pieces = [[w[kv] for w in walked] + [swapped[kv]] for kv in range(2)]
    z = r // 4
    o = (wanted // 4 - z) % n_z
    p0 = jnp.where(o == 0, 0, jnp.where(o >= reach, n_z - o, reach + o))
    p1 = jnp.where(o <= reach, o, reach + n_z - o)
    return pieces, jnp.where(core == 0, p0, p1) * 4 + wanted % 4


def attend_kernel(scal_ref, q_ref, *refs, per_kv, half, n_blocks, n_pieces):
    piece_refs = (refs[:n_pieces], refs[n_pieces : 2 * n_pieces])
    s0_ref, s1_ref, o_ref, buf, sems = refs[2 * n_pieces :]
    h = pl.program_id(0)
    i = pl.program_id(1)
    base = scal_ref[0]
    start = jnp.where(h == 0, scal_ref[1], scal_ref[3])
    stop = jnp.where(h == 0, scal_ref[2], scal_ref[4])
    slot0 = base + h * half + i * TILE
    any_live = (start < slot0 + TILE) & (stop > slot0)
    rows = per_kv * TILE
    scale = 1.0 / math.sqrt(HD)
    block_rows = piece_refs[0][0].shape[1]
    group = piece_refs[0][0].shape[0]
    last = n_pieces - 1

    def dst(hh, kv, b):
        return buf.at[hh, kv, pl.ds(b * block_rows, block_rows), :]

    def start_copy(hh, b):
        where = scal_ref[8 + hh * n_blocks + b]
        place = where // group
        for p in range(n_pieces):
            hit = (place == p) if p < last else (place >= last)
            at = where % group if p < last else where - last * group

            @pl.when(hit)
            def _():
                for kv in range(2):
                    pltpu.make_async_copy(
                        piece_refs[kv][p].at[at], dst(hh, kv, b), sems.at[hh, kv, b]
                    ).start()

    def wait_copy(hh, b):
        for kv in range(2):
            pltpu.make_async_copy(
                piece_refs[kv][0].at[0], dst(hh, kv, b), sems.at[hh, kv, b]
            ).wait()

    @pl.when((h == 0) & (i == 0))
    def _():
        for hh in range(2):
            for b in range(n_blocks):
                start_copy(hh, b)

    @pl.when(jnp.logical_not(any_live))
    def _():
        o_ref[...] = jnp.zeros_like(o_ref)

    def body(hh, s_ref, key_base, n_suffix):
        @pl.when(i == 0)
        def _():
            for b in range(n_blocks):
                wait_copy(hh, b)

        @pl.when(any_live)
        def _():
            compute(hh, s_ref, key_base, n_suffix)

    def compute(hh, s_ref, key_base, n_suffix):
        kref = buf.at[hh, 0]
        vref = buf.at[hh, 1]
        q = jnp.concatenate([q_ref[:, j * HD : (j + 1) * HD] for j in range(per_kv)], axis=0)
        row = lax.broadcasted_iota(jnp.int32, (rows, 1), 0)
        slot = slot0 + jnp.bitwise_and(row, TILE - 1)
        live = (slot >= start) & (slot < stop)
        key_slot = key_base + lax.broadcasted_iota(jnp.int32, (1, n_suffix), 1)
        suffix_ok = (key_slot >= start) & (key_slot <= slot) & live

        def raw(k):
            return lax.dot_general(
                q, k, (((1,), (1,)), ((), ())), preferred_element_type=jnp.float32
            )

        n_chunks = kref.shape[0] // CHUNK

        def max_step(c, m):
            s = raw(kref[pl.ds(pl.multiple_of(c * CHUNK, CHUNK), CHUNK), :])
            return jnp.maximum(m, jnp.max(s, axis=1, keepdims=True))

        m = jnp.full((rows, 1), masked_score, jnp.float32)
        m = lax.fori_loop(0, n_chunks, max_step, m)
        s_suf = raw(s_ref[0]) * scale
        m = jnp.maximum(m * scale, jnp.max(jnp.where(suffix_ok, s_suf, masked_score), axis=1, keepdims=True))

        def sum_step(c, carry):
            l, acc = carry
            at = pl.ds(pl.multiple_of(c * CHUNK, CHUNK), CHUNK)
            p = jnp.exp(raw(kref[at, :]) * scale - m)
            l = l + jnp.sum(p, axis=1, keepdims=True)
            acc = acc + jnp.dot(
                p.astype(jnp.bfloat16), vref[at, :], preferred_element_type=jnp.float32
            )
            return (l, acc)

        l = jnp.zeros((rows, 1), jnp.float32)
        acc = jnp.zeros((rows, HD), jnp.float32)
        l, acc = lax.fori_loop(0, n_chunks, sum_step, (l, acc))
        p = jnp.where(suffix_ok, jnp.exp(s_suf - m), 0.0)
        l = l + jnp.sum(p, axis=1, keepdims=True)
        acc = acc + jnp.dot(p.astype(jnp.bfloat16), s_ref[1], preferred_element_type=jnp.float32)
        out = jnp.where(live, acc / jnp.where(live, l, 1.0), 0.0).astype(o_ref.dtype)
        for j in range(per_kv):
            o_ref[:, j * HD : (j + 1) * HD] = out[j * TILE : (j + 1) * TILE, :]

    @pl.when(h == 0)
    def _():
        body(0, s0_ref, base - half, s0_ref.shape[1])

    @pl.when(h == 1)
    def _():
        body(1, s1_ref, base + half, s1_ref.shape[1])


def per_device(
    queries, suffix_kv, prefix_kv, suffix_length, request_group, request_order, owner_map
):
    tok_rows = queries.shape[0]
    head_cols = suffix_kv.shape[2]
    kv_heads = head_cols // HD
    per_kv = queries.shape[1] // head_cols
    stored_count = owner_map.shape[0]
    per_group = stored_count // GROUPS
    requests = suffix_length.shape[0]
    half = tok_rows // 2
    packed_length = jnp.take(suffix_length, request_order)
    packed_group = jnp.take(request_group, request_order)
    starts = (jnp.arange(requests, dtype=jnp.int32) + 1) * tok_rows - packed_length // 2
    stops = starts + packed_length
    device = lax.axis_index("req")
    base = device * tok_rows
    first = jnp.clip(device - 1, 0, requests - 1)
    second = jnp.clip(device, 0, requests - 1)
    has_first = device >= 1
    has_second = device < requests
    start0 = jnp.where(has_first, starts[first], -1)
    stop0 = jnp.where(has_first, stops[first], -1)
    start1 = jnp.where(has_second, starts[second], -1)
    stop1 = jnp.where(has_second, stops[second], -1)
    groups = jnp.stack([packed_group[first], packed_group[second]])
    rows_of = jnp.take(
        owner_map, groups[:, None] * per_group + jnp.arange(per_group, dtype=jnp.int32)[None, :]
    )
    head = jnp.stack([base, start0, stop0, start1, stop1, base, base, base])

    local = lax.all_to_all(prefix_kv, "tp", split_axis=3, concat_axis=2, tiled=True)
    pieces, where_block = ring_gather(local, rows_of.reshape(-1))
    scal = jnp.concatenate([head, where_block]).astype(jnp.int32)
    earlier = from_behind(suffix_kv[:, half:, :], "req", 1)
    s0 = jnp.concatenate([earlier, suffix_kv[:, :half, :]], axis=1)
    pad = (-half) % 128
    s1 = jnp.concatenate(
        [suffix_kv[:, half:, :], jnp.zeros((2, pad, head_cols), suffix_kv.dtype)], axis=1
    )

    tiles_per_half = half // TILE
    grid = (2, tiles_per_half)
    n_pieces = len(pieces[0])
    kernel = functools.partial(
        attend_kernel, per_kv=per_kv, half=half, n_blocks=per_group, n_pieces=n_pieces
    )
    block_rows = pieces[0][0].shape[1]
    prefix_rows = per_group * block_rows
    tile_map = lambda h, i, s: (h * tiles_per_half + i, 0)
    return pl.pallas_call(
        kernel,
        out_shape=jax.ShapeDtypeStruct((tok_rows, per_kv * HD), queries.dtype),
        grid_spec=pltpu.PrefetchScalarGridSpec(
            num_scalar_prefetch=1,
            grid=grid,
            in_specs=[
                pl.BlockSpec((TILE, per_kv * HD), tile_map),
                *[pl.BlockSpec(memory_space=pl.ANY)] * (2 * n_pieces),
                pl.BlockSpec(s0.shape, lambda h, i, s: (0, 0, 0)),
                pl.BlockSpec(s1.shape, lambda h, i, s: (0, 0, 0)),
            ],
            out_specs=pl.BlockSpec((TILE, per_kv * HD), tile_map),
            scratch_shapes=[
                pltpu.VMEM((2, 2, prefix_rows, HD), queries.dtype),
                pltpu.SemaphoreType.DMA((2, 2, per_group)),
            ],
        ),
        compiler_params=pltpu.CompilerParams(dimension_semantics=("arbitrary", "arbitrary")),
    )(scal, queries, *pieces[0], *pieces[1], s0, s1)


def solution(mesh):
    in_specs = (
        P("req", "tp"),
        P(None, "req", "tp"),
        P(None, "req", "tp", None),
        P(),
        P(),
        P(),
        P(),
    )
    out_specs = P("req", "tp")
    return jax.shard_map(
        per_device, mesh=mesh, in_specs=in_specs, out_specs=out_specs, check_vma=False
    )
```

```python
import functools
import math

import jax
import jax.numpy as jnp
from jax import lax
from jax.experimental import pallas as pl
from jax.experimental.pallas import tpu as pltpu
from jax.sharding import PartitionSpec as P

QH = 64
KVH = 8
HD = 128
GROUPS = 4

masked_score = -1e30
TILE = 64
WINDOW = 256


def from_behind(block, axis, distance):
    devices = range(lax.axis_size(axis))
    route = [(i - distance, i) for i in devices if i - distance in devices]
    return lax.ppermute(block, axis, route)


def ring_gather(block):
    n = lax.axis_size("req")
    r = lax.axis_index("req")
    core = r % 2
    pair = (r // 2) % 2
    reach = n // 8

    def route(fn):
        return [(i, fn(i) % n) for i in range(n)]

    def both(x, fn):
        return [lax.ppermute(x[kv], "req", route(fn)) for kv in range(2)]

    other = lax.ppermute(block, "req", route(lambda i: i ^ 1))
    two = jnp.where(core == 0, jnp.concatenate([block, other], 1), jnp.concatenate([other, block], 1))
    two = [two[0], two[1]]
    other = both(two, lambda i: i ^ 2)
    four = [
        jnp.where(pair == 0, jnp.concatenate([t, o], 0), jnp.concatenate([o, t], 0))
        for t, o in zip(two, other)
    ]
    walked = [four]
    for _ in range(reach):
        walked.append(both(walked[-1], lambda i: i + 4 if i % 2 == 0 else i - 4))
    mine = [jnp.concatenate([w[kv] for w in walked[1:reach]], 0) for kv in range(2)]
    swapped = both(mine, lambda i: i ^ 1)
    return [[w[kv] for w in walked] + [swapped[kv]] for kv in range(2)]


def attend_kernel(
    len_ref, group_ref, order_ref, owner_ref, q_ref, *refs,
    per_kv, half, n_blocks, n_pieces, n_dev, requests, tok_rows
):
    piece_refs = (refs[:n_pieces], refs[n_pieces : 2 * n_pieces])
    prev_ref, own_ref, o_ref, buf, sems = refs[2 * n_pieces :]
    h = pl.program_id(0)
    i = pl.program_id(1)
    r = lax.axis_index("req")
    base = r * tok_rows

    def span(k):
        length = len_ref[order_ref[k]]
        first = (k + 1) * tok_rows - length // 2
        return first, first + length

    k0 = jnp.maximum(r - 1, 0)
    k1 = jnp.minimum(r, requests - 1)
    start0, stop0 = span(k0)
    start1, stop1 = span(k1)
    start0 = jnp.where(r >= 1, start0, -1)
    stop0 = jnp.where(r >= 1, stop0, -1)
    start1 = jnp.where(r < requests, start1, -1)
    stop1 = jnp.where(r < requests, stop1, -1)
    start = jnp.where(h == 0, start0, start1)
    stop = jnp.where(h == 0, stop0, stop1)
    slot0 = base + h * half + i * TILE
    any_live = (start < slot0 + TILE) & (stop > slot0)
    rows = per_kv * TILE
    scale = 1.0 / math.sqrt(HD)
    block_rows = piece_refs[0][0].shape[1]
    group = piece_refs[0][0].shape[0]
    last = n_pieces - 1
    n_z = n_dev // 4
    reach = n_z // 2
    core = r % 2
    z = r // 4

    def position(hh, b):
        g = group_ref[order_ref[k0 if hh == 0 else k1]]
        d = owner_ref[g * n_blocks + b]
        o = (d // 4 - z + n_z) % n_z
        p0 = jnp.where(o == 0, 0, jnp.where(o >= reach, n_z - o, reach + o))
        p1 = jnp.where(o <= reach, o, reach + n_z - o)
        return jnp.where(core == 0, p0, p1) * 4 + d % 4

    def dst(hh, kv, b):
        return buf.at[hh, kv, pl.ds(b * block_rows, block_rows), :]

    def start_copy(hh, b):
        where = position(hh, b)
        place = where // group
        for p in range(n_pieces):
            hit = (place == p) if p < last else (place >= last)
            at = where % group if p < last else where - last * group

            @pl.when(hit)
            def _():
                for kv in range(2):
                    pltpu.make_async_copy(
                        piece_refs[kv][p].at[at], dst(hh, kv, b), sems.at[hh, kv, b]
                    ).start()

    def wait_copy(hh, b):
        for kv in range(2):
            pltpu.make_async_copy(
                piece_refs[kv][0].at[0], dst(hh, kv, b), sems.at[hh, kv, b]
            ).wait()

    @pl.when((h == 0) & (i == 0))
    def _():
        for hh in range(2):
            for b in range(n_blocks):
                start_copy(hh, b)

    @pl.when(jnp.logical_not(any_live))
    def _():
        o_ref[...] = jnp.zeros_like(o_ref)

    def body(hh, chunks):
        @pl.when(i == 0)
        def _():
            for b in range(n_blocks):
                wait_copy(hh, b)

        @pl.when(any_live)
        def _():
            compute(hh, chunks)

    def compute(hh, chunks):
        kref = buf.at[hh, 0]
        vref = buf.at[hh, 1]
        q = jnp.concatenate([q_ref[:, j * HD : (j + 1) * HD] for j in range(per_kv)], axis=0)
        row = lax.broadcasted_iota(jnp.int32, (rows, 1), 0)
        slot = slot0 + jnp.bitwise_and(row, TILE - 1)
        live = (slot >= start) & (slot < stop)

        def raw(k):
            return lax.dot_general(
                q, k, (((1,), (1,)), ((), ())), preferred_element_type=jnp.float32
            )

        s_pre = raw(kref[...])
        m = jnp.max(s_pre, axis=1, keepdims=True) * scale
        suffix = []
        for kc, vc, key_base in chunks:
            key_slot = key_base + lax.broadcasted_iota(jnp.int32, (1, kc.shape[0]), 1)
            ok = (key_slot >= start) & (key_slot <= slot) & live
            s = raw(kc) * scale
            m = jnp.maximum(m, jnp.max(jnp.where(ok, s, masked_score), axis=1, keepdims=True))
            suffix.append((s, ok, vc))
        p = jnp.exp(s_pre * scale - m)
        l = jnp.sum(p, axis=1, keepdims=True)
        acc = jnp.dot(p.astype(jnp.bfloat16), vref[...], preferred_element_type=jnp.float32)
        for s, ok, vc in suffix:
            p = jnp.where(ok, jnp.exp(s - m), 0.0)
            l = l + jnp.sum(p, axis=1, keepdims=True)
            acc = acc + jnp.dot(p.astype(jnp.bfloat16), vc, preferred_element_type=jnp.float32)
        out = jnp.where(live, acc / jnp.where(live, l, 1.0), 0.0).astype(o_ref.dtype)
        for j in range(per_kv):
            o_ref[:, j * HD : (j + 1) * HD] = out[j * TILE : (j + 1) * TILE, :]

    skip = tok_rows - WINDOW

    @pl.when(h == 0)
    def _():
        body(
            0,
            [
                (prev_ref[0], prev_ref[1], base - WINDOW),
                (own_ref[0, :WINDOW], own_ref[1, :WINDOW], base),
            ],
        )

    @pl.when(h == 1)
    def _():
        body(1, [(own_ref[0, skip:], own_ref[1, skip:], base + skip)])


def per_device(
    queries, suffix_kv, prefix_kv, suffix_length, request_group, request_order, owner_map
):
    tok_rows = queries.shape[0]
    head_cols = suffix_kv.shape[2]
    per_kv = queries.shape[1] // head_cols
    stored_count = owner_map.shape[0]
    per_group = stored_count // GROUPS
    requests = suffix_length.shape[0]
    half = tok_rows // 2

    local = lax.all_to_all(prefix_kv, "tp", split_axis=3, concat_axis=2, tiled=True)
    pieces = ring_gather(local)
    earlier = from_behind(suffix_kv[:, tok_rows - WINDOW :, :], "req", 1)

    tiles_per_half = half // TILE
    grid = (2, tiles_per_half)
    n_pieces = len(pieces[0])
    kernel = functools.partial(
        attend_kernel,
        per_kv=per_kv,
        half=half,
        n_blocks=per_group,
        n_pieces=n_pieces,
        n_dev=lax.axis_size("req"),
        requests=requests,
        tok_rows=tok_rows,
    )
    block_rows = pieces[0][0].shape[1]
    prefix_rows = per_group * block_rows
    tile_map = lambda h, i, *s: (h * tiles_per_half + i, 0)
    whole = lambda h, i, *s: (0, 0, 0)
    return pl.pallas_call(
        kernel,
        out_shape=jax.ShapeDtypeStruct((tok_rows, per_kv * HD), queries.dtype),
        grid_spec=pltpu.PrefetchScalarGridSpec(
            num_scalar_prefetch=4,
            grid=grid,
            in_specs=[
                pl.BlockSpec((TILE, per_kv * HD), tile_map),
                *[pl.BlockSpec(memory_space=pl.ANY)] * (2 * n_pieces),
                pl.BlockSpec(earlier.shape, whole),
                pl.BlockSpec(suffix_kv.shape, whole),
            ],
            out_specs=pl.BlockSpec((TILE, per_kv * HD), tile_map),
            scratch_shapes=[
                pltpu.VMEM((2, 2, prefix_rows, HD), queries.dtype),
                pltpu.SemaphoreType.DMA((2, 2, per_group)),
            ],
        ),
        compiler_params=pltpu.CompilerParams(dimension_semantics=("arbitrary", "arbitrary")),
    )(
        suffix_length,
        request_group,
        request_order,
        owner_map,
        queries,
        *pieces[0],
        *pieces[1],
        earlier,
        suffix_kv,
    )


def solution(mesh):
    in_specs = (
        P("req", "tp"),
        P(None, "req", "tp"),
        P(None, "req", "tp", None),
        P(),
        P(),
        P(),
        P(),
    )
    out_specs = P("req", "tp")
    return jax.shard_map(
        per_device, mesh=mesh, in_specs=in_specs, out_specs=out_specs, check_vma=False
    )
```

```python
import functools
import math

import jax
import jax.numpy as jnp
from jax import lax
from jax.experimental import pallas as pl
from jax.experimental.pallas import tpu as pltpu
from jax.sharding import PartitionSpec as P

QH = 64
KVH = 8
HD = 128
GROUPS = 4

masked_score = -1e30
TILE = 64
WINDOW = 256


def from_behind(block, axis, distance):
    devices = range(lax.axis_size(axis))
    route = [(i - distance, i) for i in devices if i - distance in devices]
    return lax.ppermute(block, axis, route)


def ring_gather(block):
    n = lax.axis_size("req")
    r = lax.axis_index("req")
    core = r % 2
    pair = (r // 2) % 2
    reach = n // 8

    def route(fn):
        return [(i, fn(i) % n) for i in range(n)]

    def both(x, fn):
        return [lax.ppermute(x[kv], "req", route(fn)) for kv in range(2)]

    other = lax.ppermute(block, "req", route(lambda i: i ^ 1))
    two = jnp.where(core == 0, jnp.concatenate([block, other], 1), jnp.concatenate([other, block], 1))
    two = [two[0], two[1]]
    other = both(two, lambda i: i ^ 2)
    four = [
        jnp.where(pair == 0, jnp.concatenate([t, o], 0), jnp.concatenate([o, t], 0))
        for t, o in zip(two, other)
    ]
    walked = [four]
    for _ in range(reach):
        walked.append(both(walked[-1], lambda i: i + 4 if i % 2 == 0 else i - 4))
    mine = [jnp.concatenate([w[kv] for w in walked[1:reach]], 0) for kv in range(2)]
    swapped = both(mine, lambda i: i ^ 1)
    return [[w[kv] for w in walked] + [swapped[kv]] for kv in range(2)]


def attend_kernel(
    len_ref, group_ref, order_ref, owner_ref, q_ref, *refs,
    per_kv, half, n_blocks, n_pieces, n_dev, requests, tok_rows
):
    piece_refs = (refs[:n_pieces], refs[n_pieces : 2 * n_pieces])
    prev_ref, own_ref, o_ref, buf, sems = refs[2 * n_pieces :]
    h = pl.program_id(0)
    i = pl.program_id(1)
    r = lax.axis_index("req")
    base = r * tok_rows

    def span(k):
        length = len_ref[order_ref[k]]
        first = (k + 1) * tok_rows - length // 2
        return first, first + length

    k0 = jnp.maximum(r - 1, 0)
    k1 = jnp.minimum(r, requests - 1)
    start0, stop0 = span(k0)
    start1, stop1 = span(k1)
    start0 = jnp.where(r >= 1, start0, -1)
    stop0 = jnp.where(r >= 1, stop0, -1)
    start1 = jnp.where(r < requests, start1, -1)
    stop1 = jnp.where(r < requests, stop1, -1)
    start = jnp.where(h == 0, start0, start1)
    stop = jnp.where(h == 0, stop0, stop1)
    slot0 = base + h * half + i * TILE
    any_live = (start < slot0 + TILE) & (stop > slot0)
    rows = per_kv * TILE
    scale = 1.0 / math.sqrt(HD)
    block_rows = piece_refs[0][0].shape[1]
    group = piece_refs[0][0].shape[0]
    last = n_pieces - 1
    n_z = n_dev // 4
    reach = n_z // 2
    core = r % 2
    z = r // 4

    def position(hh, b):
        g = group_ref[order_ref[k0 if hh == 0 else k1]]
        d = owner_ref[g * n_blocks + b]
        o = (d // 4 - z + n_z) % n_z
        p0 = jnp.where(o == 0, 0, jnp.where(o >= reach, n_z - o, reach + o))
        p1 = jnp.where(o <= reach, o, reach + n_z - o)
        return jnp.where(core == 0, p0, p1) * 4 + d % 4

    def dst(hh, kv, b):
        return buf.at[hh, kv, pl.ds(b * block_rows, block_rows), :]

    def start_copy(hh, b):
        where = position(hh, b)
        place = where // group
        for p in range(n_pieces):
            hit = (place == p) if p < last else (place >= last)
            at = where % group if p < last else where - last * group

            @pl.when(hit)
            def _():
                for kv in range(2):
                    pltpu.make_async_copy(
                        piece_refs[kv][p].at[at], dst(hh, kv, b), sems.at[hh, kv, b]
                    ).start()

    def wait_copy(hh, b):
        for kv in range(2):
            pltpu.make_async_copy(
                piece_refs[kv][0].at[0], dst(hh, kv, b), sems.at[hh, kv, b]
            ).wait()

    @pl.when((h == 0) & (i == 0))
    def _():
        for hh in range(2):
            for b in range(n_blocks):
                start_copy(hh, b)

    @pl.when(jnp.logical_not(any_live))
    def _():
        o_ref[...] = jnp.zeros_like(o_ref)

    def body(hh, chunks):
        @pl.when(i == 0)
        def _():
            for b in range(n_blocks):
                wait_copy(hh, b)

        @pl.when(any_live)
        def _():
            compute(hh, chunks)

    def compute(hh, chunks):
        kref = buf.at[hh, 0]
        vref = buf.at[hh, 1]
        q = jnp.concatenate([q_ref[:, j * HD : (j + 1) * HD] for j in range(per_kv)], axis=0)
        row = lax.broadcasted_iota(jnp.int32, (rows, 1), 0)
        slot = slot0 + jnp.bitwise_and(row, TILE - 1)
        live = (slot >= start) & (slot < stop)

        def raw(k):
            return lax.dot_general(
                q, k, (((1,), (1,)), ((), ())), preferred_element_type=jnp.float32
            )

        s_pre = raw(kref[...])
        m = jnp.max(s_pre, axis=1, keepdims=True) * scale
        suffix = []
        for kc, vc, key_base in chunks:
            key_slot = key_base + lax.broadcasted_iota(jnp.int32, (1, kc.shape[0]), 1)
            ok = (key_slot >= start) & (key_slot <= slot) & live
            s = raw(kc) * scale
            m = jnp.maximum(m, jnp.max(jnp.where(ok, s, masked_score), axis=1, keepdims=True))
            suffix.append((s, ok, vc))
        p = jnp.exp(s_pre * scale - m)
        l = jnp.sum(p, axis=1, keepdims=True)
        acc = jnp.dot(p.astype(jnp.bfloat16), vref[...], preferred_element_type=jnp.float32)
        for s, ok, vc in suffix:
            p = jnp.where(ok, jnp.exp(s - m), 0.0)
            l = l + jnp.sum(p, axis=1, keepdims=True)
            acc = acc + jnp.dot(p.astype(jnp.bfloat16), vc, preferred_element_type=jnp.float32)
        out = jnp.where(live, acc / jnp.where(live, l, 1.0), 0.0).astype(o_ref.dtype)
        for j in range(per_kv):
            o_ref[:, j * HD : (j + 1) * HD] = out[j * TILE : (j + 1) * TILE, :]

    skip = tok_rows - WINDOW

    @pl.when(h == 0)
    def _():
        body(
            0,
            [
                (prev_ref[0], prev_ref[1], base - WINDOW),
                (own_ref[0, :WINDOW], own_ref[1, :WINDOW], base),
            ],
        )

    @pl.when(h == 1)
    def _():
        body(1, [(own_ref[0, skip:], own_ref[1, skip:], base + skip)])


def per_device(
    queries, suffix_kv, prefix_kv, suffix_length, request_group, request_order, owner_map
):
    tok_rows = queries.shape[0]
    head_cols = suffix_kv.shape[2]
    per_kv = queries.shape[1] // head_cols
    stored_count = owner_map.shape[0]
    per_group = stored_count // GROUPS
    requests = suffix_length.shape[0]
    half = tok_rows // 2

    earlier = from_behind(suffix_kv[:, tok_rows - WINDOW :, :], "req", 1)
    local = lax.all_to_all(prefix_kv, "tp", split_axis=3, concat_axis=2, tiled=True)
    local, earlier = lax.optimization_barrier((local, earlier))
    pieces = ring_gather(local)

    tiles_per_half = half // TILE
    grid = (2, tiles_per_half)
    n_pieces = len(pieces[0])
    kernel = functools.partial(
        attend_kernel,
        per_kv=per_kv,
        half=half,
        n_blocks=per_group,
        n_pieces=n_pieces,
        n_dev=lax.axis_size("req"),
        requests=requests,
        tok_rows=tok_rows,
    )
    block_rows = pieces[0][0].shape[1]
    prefix_rows = per_group * block_rows
    tile_map = lambda h, i, *s: (h * tiles_per_half + i, 0)
    whole = lambda h, i, *s: (0, 0, 0)
    return pl.pallas_call(
        kernel,
        out_shape=jax.ShapeDtypeStruct((tok_rows, per_kv * HD), queries.dtype),
        grid_spec=pltpu.PrefetchScalarGridSpec(
            num_scalar_prefetch=4,
            grid=grid,
            in_specs=[
                pl.BlockSpec((TILE, per_kv * HD), tile_map),
                *[pl.BlockSpec(memory_space=pl.ANY)] * (2 * n_pieces),
                pl.BlockSpec(earlier.shape, whole),
                pl.BlockSpec(suffix_kv.shape, whole),
            ],
            out_specs=pl.BlockSpec((TILE, per_kv * HD), tile_map),
            scratch_shapes=[
                pltpu.VMEM((2, 2, prefix_rows, HD), queries.dtype),
                pltpu.SemaphoreType.DMA((2, 2, per_group)),
            ],
        ),
        compiler_params=pltpu.CompilerParams(dimension_semantics=("arbitrary", "arbitrary")),
    )(
        suffix_length,
        request_group,
        request_order,
        owner_map,
        queries,
        *pieces[0],
        *pieces[1],
        earlier,
        suffix_kv,
    )


def solution(mesh):
    in_specs = (
        P("req", "tp"),
        P(None, "req", "tp"),
        P(None, "req", "tp", None),
        P(),
        P(),
        P(),
        P(),
    )
    out_specs = P("req", "tp")
    return jax.shard_map(
        per_device, mesh=mesh, in_specs=in_specs, out_specs=out_specs, check_vma=False
    )
```

```python
import functools
import math

import jax
import jax.numpy as jnp
from jax import lax
from jax.experimental import pallas as pl
from jax.experimental.pallas import tpu as pltpu
from jax.sharding import PartitionSpec as P

QH = 64
KVH = 8
HD = 128
GROUPS = 4

masked_score = -1e30
TILE = 64
WINDOW = 256


def from_behind(block, axis, distance):
    devices = range(lax.axis_size(axis))
    route = [(i - distance, i) for i in devices if i - distance in devices]
    return lax.ppermute(block, axis, route)


def ring_gather(block):
    n = lax.axis_size("req")
    r = lax.axis_index("req")
    core = r % 2
    pair = (r // 2) % 2
    reach = n // 8

    def route(fn):
        return [(i, fn(i) % n) for i in range(n)]

    def both(x, fn):
        return [lax.ppermute(x[kv], "req", route(fn)) for kv in range(2)]

    other = lax.ppermute(block, "req", route(lambda i: i ^ 1))
    two = jnp.where(core == 0, jnp.concatenate([block, other], 1), jnp.concatenate([other, block], 1))
    two = [two[0], two[1]]
    other = both(two, lambda i: i ^ 2)
    four = [
        jnp.where(pair == 0, jnp.concatenate([t, o], 0), jnp.concatenate([o, t], 0))
        for t, o in zip(two, other)
    ]
    walked = [four]
    for _ in range(reach - 1):
        walked.append(both(walked[-1], lambda i: i + 4 if i % 2 == 0 else i - 4))
    walked.append(
        [
            lax.ppermute(walked[-1][0], "req", [(i, (i + 4) % n) for i in range(0, n, 2)]),
            lax.ppermute(walked[-1][1], "req", [(i, (i - 4) % n) for i in range(1, n, 2)]),
        ]
    )
    mine = [jnp.concatenate([w[kv] for w in walked[1:]], 0) for kv in range(2)]
    swapped = both(mine, lambda i: i ^ 1)
    return [[w[kv] for w in walked] + [swapped[kv]] for kv in range(2)]


def attend_kernel(
    len_ref, group_ref, order_ref, owner_ref, q_ref, *refs,
    per_kv, half, n_blocks, n_pieces, n_dev, requests, tok_rows
):
    piece_refs = (refs[:n_pieces], refs[n_pieces : 2 * n_pieces])
    prev_ref, own_ref, o_ref, buf, sems = refs[2 * n_pieces :]
    h = pl.program_id(0)
    i = pl.program_id(1)
    r = lax.axis_index("req")
    base = r * tok_rows

    def span(k):
        length = len_ref[order_ref[k]]
        first = (k + 1) * tok_rows - length // 2
        return first, first + length

    k0 = jnp.maximum(r - 1, 0)
    k1 = jnp.minimum(r, requests - 1)
    start0, stop0 = span(k0)
    start1, stop1 = span(k1)
    start0 = jnp.where(r >= 1, start0, -1)
    stop0 = jnp.where(r >= 1, stop0, -1)
    start1 = jnp.where(r < requests, start1, -1)
    stop1 = jnp.where(r < requests, stop1, -1)
    start = jnp.where(h == 0, start0, start1)
    stop = jnp.where(h == 0, stop0, stop1)
    slot0 = base + h * half + i * TILE
    any_live = (start < slot0 + TILE) & (stop > slot0)
    rows = per_kv * TILE
    scale = 1.0 / math.sqrt(HD)
    block_rows = piece_refs[0][0].shape[1]
    group = piece_refs[0][0].shape[0]
    last = n_pieces - 1
    n_z = n_dev // 4
    reach = n_z // 2
    core = r % 2
    z = r // 4

    def position(hh, b):
        g = group_ref[order_ref[k0 if hh == 0 else k1]]
        d = owner_ref[g * n_blocks + b]
        o = (d // 4 - z + n_z) % n_z
        p0 = jnp.where(o == 0, 0, jnp.where(o >= reach, n_z - o, reach + o))
        p1 = jnp.where(o <= reach, o, reach + n_z - o)
        return jnp.where(core == 0, p0, p1) * 4 + d % 4

    def dst(hh, kv, b):
        return buf.at[hh, kv, pl.ds(b * block_rows, block_rows), :]

    def copy(kv, p, at, hh, b):
        pltpu.make_async_copy(
            piece_refs[kv][p].at[at], dst(hh, kv, b), sems.at[hh, kv, b]
        ).start()

    def start_copy(hh, b):
        where = position(hh, b)
        place = where // group
        j = where % group
        for p in range(reach):

            @pl.when(place == p)
            def _():
                for kv in range(2):
                    copy(kv, p, j, hh, b)

        tail = (reach - 1) * group + j

        @pl.when((place == reach) & (core == 0))
        def _():
            copy(0, reach, j, hh, b)
            copy(1, last, tail, hh, b)

        @pl.when((place == reach) & (core == 1))
        def _():
            copy(0, last, tail, hh, b)
            copy(1, reach, j, hh, b)

        @pl.when(place > reach)
        def _():
            for kv in range(2):
                copy(kv, last, where - (reach + 1) * group, hh, b)

    def wait_copy(hh, b):
        for kv in range(2):
            pltpu.make_async_copy(
                piece_refs[kv][0].at[0], dst(hh, kv, b), sems.at[hh, kv, b]
            ).wait()

    @pl.when((h == 0) & (i == 0))
    def _():
        for hh in range(2):
            for b in range(n_blocks):
                start_copy(hh, b)

    @pl.when(jnp.logical_not(any_live))
    def _():
        o_ref[...] = jnp.zeros_like(o_ref)

    def body(hh, chunks):
        @pl.when(i == 0)
        def _():
            for b in range(n_blocks):
                wait_copy(hh, b)

        @pl.when(any_live)
        def _():
            compute(hh, chunks)

    def compute(hh, chunks):
        kref = buf.at[hh, 0]
        vref = buf.at[hh, 1]
        q = jnp.concatenate([q_ref[:, j * HD : (j + 1) * HD] for j in range(per_kv)], axis=0)
        row = lax.broadcasted_iota(jnp.int32, (rows, 1), 0)
        slot = slot0 + jnp.bitwise_and(row, TILE - 1)
        live = (slot >= start) & (slot < stop)

        def raw(k):
            return lax.dot_general(
                q, k, (((1,), (1,)), ((), ())), preferred_element_type=jnp.float32
            )

        s_pre = raw(kref[...])
        m = jnp.max(s_pre, axis=1, keepdims=True) * scale
        suffix = []
        for kc, vc, key_base in chunks:
            key_slot = key_base + lax.broadcasted_iota(jnp.int32, (1, kc.shape[0]), 1)
            ok = (key_slot >= start) & (key_slot <= slot) & live
            s = raw(kc) * scale
            m = jnp.maximum(m, jnp.max(jnp.where(ok, s, masked_score), axis=1, keepdims=True))
            suffix.append((s, ok, vc))
        p = jnp.exp(s_pre * scale - m)
        l = jnp.sum(p, axis=1, keepdims=True)
        acc = jnp.dot(p.astype(jnp.bfloat16), vref[...], preferred_element_type=jnp.float32)
        for s, ok, vc in suffix:
            p = jnp.where(ok, jnp.exp(s - m), 0.0)
            l = l + jnp.sum(p, axis=1, keepdims=True)
            acc = acc + jnp.dot(p.astype(jnp.bfloat16), vc, preferred_element_type=jnp.float32)
        out = jnp.where(live, acc / jnp.where(live, l, 1.0), 0.0).astype(o_ref.dtype)
        for j in range(per_kv):
            o_ref[:, j * HD : (j + 1) * HD] = out[j * TILE : (j + 1) * TILE, :]

    skip = tok_rows - WINDOW

    @pl.when(h == 0)
    def _():
        body(
            0,
            [
                (prev_ref[0], prev_ref[1], base - WINDOW),
                (own_ref[0, :WINDOW], own_ref[1, :WINDOW], base),
            ],
        )

    @pl.when(h == 1)
    def _():
        body(1, [(own_ref[0, skip:], own_ref[1, skip:], base + skip)])


def per_device(
    queries, suffix_kv, prefix_kv, suffix_length, request_group, request_order, owner_map
):
    tok_rows = queries.shape[0]
    head_cols = suffix_kv.shape[2]
    per_kv = queries.shape[1] // head_cols
    stored_count = owner_map.shape[0]
    per_group = stored_count // GROUPS
    requests = suffix_length.shape[0]
    half = tok_rows // 2

    earlier = from_behind(suffix_kv[:, tok_rows - WINDOW :, :], "req", 1)
    local = lax.all_to_all(prefix_kv, "tp", split_axis=3, concat_axis=2, tiled=True)
    local, earlier = lax.optimization_barrier((local, earlier))
    pieces = ring_gather(local)

    tiles_per_half = half // TILE
    grid = (2, tiles_per_half)
    n_pieces = len(pieces[0])
    kernel = functools.partial(
        attend_kernel,
        per_kv=per_kv,
        half=half,
        n_blocks=per_group,
        n_pieces=n_pieces,
        n_dev=lax.axis_size("req"),
        requests=requests,
        tok_rows=tok_rows,
    )
    block_rows = pieces[0][0].shape[1]
    prefix_rows = per_group * block_rows
    tile_map = lambda h, i, *s: (h * tiles_per_half + i, 0)
    whole = lambda h, i, *s: (0, 0, 0)
    return pl.pallas_call(
        kernel,
        out_shape=jax.ShapeDtypeStruct((tok_rows, per_kv * HD), queries.dtype),
        grid_spec=pltpu.PrefetchScalarGridSpec(
            num_scalar_prefetch=4,
            grid=grid,
            in_specs=[
                pl.BlockSpec((TILE, per_kv * HD), tile_map),
                *[pl.BlockSpec(memory_space=pl.ANY)] * (2 * n_pieces),
                pl.BlockSpec(earlier.shape, whole),
                pl.BlockSpec(suffix_kv.shape, whole),
            ],
            out_specs=pl.BlockSpec((TILE, per_kv * HD), tile_map),
            scratch_shapes=[
                pltpu.VMEM((2, 2, prefix_rows, HD), queries.dtype),
                pltpu.SemaphoreType.DMA((2, 2, per_group)),
            ],
        ),
        compiler_params=pltpu.CompilerParams(dimension_semantics=("arbitrary", "arbitrary")),
    )(
        suffix_length,
        request_group,
        request_order,
        owner_map,
        queries,
        *pieces[0],
        *pieces[1],
        earlier,
        suffix_kv,
    )


def solution(mesh):
    in_specs = (
        P("req", "tp"),
        P(None, "req", "tp"),
        P(None, "req", "tp", None),
        P(),
        P(),
        P(),
        P(),
    )
    out_specs = P("req", "tp")
    return jax.shard_map(
        per_device, mesh=mesh, in_specs=in_specs, out_specs=out_specs, check_vma=False
    )
```

```python
import functools
import math

import jax
import jax.numpy as jnp
from jax import lax
from jax.experimental import pallas as pl
from jax.experimental.pallas import tpu as pltpu
from jax.sharding import PartitionSpec as P

QH = 64
KVH = 8
HD = 128
GROUPS = 4

masked_score = -1e30
TILE = 64
WINDOW = 256


def from_behind(block, axis, distance):
    devices = range(lax.axis_size(axis))
    route = [(i - distance, i) for i in devices if i - distance in devices]
    return lax.ppermute(block, axis, route)


def ring_gather(block):
    n = lax.axis_size("req")
    r = lax.axis_index("req")
    core = r % 2
    pair = (r // 2) % 2
    reach = n // 8

    def route(fn):
        return [(i, fn(i) % n) for i in range(n)]

    def both(x, fn):
        return [lax.ppermute(x[kv], "req", route(fn)) for kv in range(2)]

    other = lax.ppermute(block, "req", route(lambda i: i ^ 1))
    two = jnp.where(core == 0, jnp.concatenate([block, other], 1), jnp.concatenate([other, block], 1))
    two = [two[0], two[1]]
    other = both(two, lambda i: i ^ 2)
    four = [
        jnp.where(pair == 0, jnp.concatenate([t, o], 0), jnp.concatenate([o, t], 0))
        for t, o in zip(two, other)
    ]
    walked = [four]
    for _ in range(reach - 1):
        walked.append(both(walked[-1], lambda i: i + 4 if i % 2 == 0 else i - 4))
    walked.append(
        [
            lax.ppermute(walked[-1][0], "req", [(i, (i + 4) % n) for i in range(0, n, 2)]),
            lax.ppermute(walked[-1][1], "req", [(i, (i - 4) % n) for i in range(1, n, 2)]),
        ]
    )
    mine = [jnp.concatenate([w[kv] for w in walked[1:reach]], 0) for kv in range(2)]
    swapped = both(mine, lambda i: i ^ 1)
    extra = [
        lax.ppermute(walked[reach][0], "req", [(i, i + 1) for i in range(0, n, 2)]),
        lax.ppermute(walked[reach][1], "req", [(i, i - 1) for i in range(1, n, 2)]),
    ]
    return [[w[kv] for w in walked] + [swapped[kv], extra[kv]] for kv in range(2)]


def attend_kernel(
    len_ref, group_ref, order_ref, owner_ref, q_ref, *refs,
    per_kv, half, n_blocks, n_pieces, n_dev, requests, tok_rows
):
    piece_refs = (refs[:n_pieces], refs[n_pieces : 2 * n_pieces])
    prev_ref, own_ref, o_ref, buf, sems = refs[2 * n_pieces :]
    h = pl.program_id(0)
    i = pl.program_id(1)
    r = lax.axis_index("req")
    base = r * tok_rows

    def span(k):
        length = len_ref[order_ref[k]]
        first = (k + 1) * tok_rows - length // 2
        return first, first + length

    k0 = jnp.maximum(r - 1, 0)
    k1 = jnp.minimum(r, requests - 1)
    start0, stop0 = span(k0)
    start1, stop1 = span(k1)
    start0 = jnp.where(r >= 1, start0, -1)
    stop0 = jnp.where(r >= 1, stop0, -1)
    start1 = jnp.where(r < requests, start1, -1)
    stop1 = jnp.where(r < requests, stop1, -1)
    start = jnp.where(h == 0, start0, start1)
    stop = jnp.where(h == 0, stop0, stop1)
    slot0 = base + h * half + i * TILE
    any_live = (start < slot0 + TILE) & (stop > slot0)
    rows = per_kv * TILE
    scale = 1.0 / math.sqrt(HD)
    block_rows = piece_refs[0][0].shape[1]
    group = piece_refs[0][0].shape[0]
    last = n_pieces - 1
    n_z = n_dev // 4
    reach = n_z // 2
    core = r % 2
    z = r // 4

    def position(hh, b):
        g = group_ref[order_ref[k0 if hh == 0 else k1]]
        d = owner_ref[g * n_blocks + b]
        o = (d // 4 - z + n_z) % n_z
        p0 = jnp.where(o == 0, 0, jnp.where(o >= reach, n_z - o, reach + o))
        p1 = jnp.where(o <= reach, o, reach + n_z - o)
        return jnp.where(core == 0, p0, p1) * 4 + d % 4

    def dst(hh, kv, b):
        return buf.at[hh, kv, pl.ds(b * block_rows, block_rows), :]

    def copy(kv, p, at, hh, b):
        pltpu.make_async_copy(
            piece_refs[kv][p].at[at], dst(hh, kv, b), sems.at[hh, kv, b]
        ).start()

    def start_copy(hh, b):
        where = position(hh, b)
        place = where // group
        j = where % group
        for p in range(reach):

            @pl.when(place == p)
            def _():
                for kv in range(2):
                    copy(kv, p, j, hh, b)

        @pl.when((place == reach) & (core == 0))
        def _():
            copy(0, reach, j, hh, b)
            copy(1, reach + 2, j, hh, b)

        @pl.when((place == reach) & (core == 1))
        def _():
            copy(0, reach + 2, j, hh, b)
            copy(1, reach, j, hh, b)

        @pl.when(place > reach)
        def _():
            for kv in range(2):
                copy(kv, reach + 1, where - (reach + 1) * group, hh, b)

    def wait_copy(hh, b):
        for kv in range(2):
            pltpu.make_async_copy(
                piece_refs[kv][0].at[0], dst(hh, kv, b), sems.at[hh, kv, b]
            ).wait()

    @pl.when((h == 0) & (i == 0))
    def _():
        for hh in range(2):
            for b in range(n_blocks):
                start_copy(hh, b)

    @pl.when(jnp.logical_not(any_live))
    def _():
        o_ref[...] = jnp.zeros_like(o_ref)

    def body(hh, chunks):
        @pl.when(i == 0)
        def _():
            for b in range(n_blocks):
                wait_copy(hh, b)

        @pl.when(any_live)
        def _():
            compute(hh, chunks)

    def compute(hh, chunks):
        kref = buf.at[hh, 0]
        vref = buf.at[hh, 1]
        q = jnp.concatenate([q_ref[:, j * HD : (j + 1) * HD] for j in range(per_kv)], axis=0)
        row = lax.broadcasted_iota(jnp.int32, (rows, 1), 0)
        slot = slot0 + jnp.bitwise_and(row, TILE - 1)
        live = (slot >= start) & (slot < stop)

        def raw(k):
            return lax.dot_general(
                q, k, (((1,), (1,)), ((), ())), preferred_element_type=jnp.float32
            )

        s_pre = raw(kref[...])
        m = jnp.max(s_pre, axis=1, keepdims=True) * scale
        suffix = []
        for kc, vc, key_base in chunks:
            key_slot = key_base + lax.broadcasted_iota(jnp.int32, (1, kc.shape[0]), 1)
            ok = (key_slot >= start) & (key_slot <= slot) & live
            s = raw(kc) * scale
            m = jnp.maximum(m, jnp.max(jnp.where(ok, s, masked_score), axis=1, keepdims=True))
            suffix.append((s, ok, vc))
        p = jnp.exp(s_pre * scale - m)
        l = jnp.sum(p, axis=1, keepdims=True)
        acc = jnp.dot(p.astype(jnp.bfloat16), vref[...], preferred_element_type=jnp.float32)
        for s, ok, vc in suffix:
            p = jnp.where(ok, jnp.exp(s - m), 0.0)
            l = l + jnp.sum(p, axis=1, keepdims=True)
            acc = acc + jnp.dot(p.astype(jnp.bfloat16), vc, preferred_element_type=jnp.float32)
        out = jnp.where(live, acc / jnp.where(live, l, 1.0), 0.0).astype(o_ref.dtype)
        for j in range(per_kv):
            o_ref[:, j * HD : (j + 1) * HD] = out[j * TILE : (j + 1) * TILE, :]

    skip = tok_rows - WINDOW

    @pl.when(h == 0)
    def _():
        body(
            0,
            [
                (prev_ref[0], prev_ref[1], base - WINDOW),
                (own_ref[0, :WINDOW], own_ref[1, :WINDOW], base),
            ],
        )

    @pl.when(h == 1)
    def _():
        body(1, [(own_ref[0, skip:], own_ref[1, skip:], base + skip)])


def per_device(
    queries, suffix_kv, prefix_kv, suffix_length, request_group, request_order, owner_map
):
    tok_rows = queries.shape[0]
    head_cols = suffix_kv.shape[2]
    per_kv = queries.shape[1] // head_cols
    stored_count = owner_map.shape[0]
    per_group = stored_count // GROUPS
    requests = suffix_length.shape[0]
    half = tok_rows // 2

    earlier = from_behind(suffix_kv[:, tok_rows - WINDOW :, :], "req", 1)
    local = lax.all_to_all(prefix_kv, "tp", split_axis=3, concat_axis=2, tiled=True)
    local, earlier = lax.optimization_barrier((local, earlier))
    pieces = ring_gather(local)

    tiles_per_half = half // TILE
    grid = (2, tiles_per_half)
    n_pieces = len(pieces[0])
    kernel = functools.partial(
        attend_kernel,
        per_kv=per_kv,
        half=half,
        n_blocks=per_group,
        n_pieces=n_pieces,
        n_dev=lax.axis_size("req"),
        requests=requests,
        tok_rows=tok_rows,
    )
    block_rows = pieces[0][0].shape[1]
    prefix_rows = per_group * block_rows
    tile_map = lambda h, i, *s: (h * tiles_per_half + i, 0)
    whole = lambda h, i, *s: (0, 0, 0)
    return pl.pallas_call(
        kernel,
        out_shape=jax.ShapeDtypeStruct((tok_rows, per_kv * HD), queries.dtype),
        grid_spec=pltpu.PrefetchScalarGridSpec(
            num_scalar_prefetch=4,
            grid=grid,
            in_specs=[
                pl.BlockSpec((TILE, per_kv * HD), tile_map),
                *[pl.BlockSpec(memory_space=pl.ANY)] * (2 * n_pieces),
                pl.BlockSpec(earlier.shape, whole),
                pl.BlockSpec(suffix_kv.shape, whole),
            ],
            out_specs=pl.BlockSpec((TILE, per_kv * HD), tile_map),
            scratch_shapes=[
                pltpu.VMEM((2, 2, prefix_rows, HD), queries.dtype),
                pltpu.SemaphoreType.DMA((2, 2, per_group)),
            ],
        ),
        compiler_params=pltpu.CompilerParams(dimension_semantics=("arbitrary", "arbitrary")),
    )(
        suffix_length,
        request_group,
        request_order,
        owner_map,
        queries,
        *pieces[0],
        *pieces[1],
        earlier,
        suffix_kv,
    )


def solution(mesh):
    in_specs = (
        P("req", "tp"),
        P(None, "req", "tp"),
        P(None, "req", "tp", None),
        P(),
        P(),
        P(),
        P(),
    )
    out_specs = P("req", "tp")
    return jax.shard_map(
        per_device, mesh=mesh, in_specs=in_specs, out_specs=out_specs, check_vma=False
    )
```

```python
import functools
import math

import jax
import jax.numpy as jnp
from jax import lax
from jax.experimental import pallas as pl
from jax.experimental.pallas import tpu as pltpu
from jax.sharding import PartitionSpec as P

QH = 64
KVH = 8
HD = 128
GROUPS = 4

masked_score = -1e30
TILE = 64
WINDOW = 256


def from_behind(block, axis, distance):
    devices = range(lax.axis_size(axis))
    route = [(i - distance, i) for i in devices if i - distance in devices]
    return lax.ppermute(block, axis, route)


def ring_gather(block):
    n = lax.axis_size("req")
    r = lax.axis_index("req")
    core = r % 2
    pair = (r // 2) % 2
    reach = n // 8

    def route(fn):
        return [(i, fn(i) % n) for i in range(n)]

    def both(x, fn):
        return [lax.ppermute(x[kv], "req", route(fn)) for kv in range(2)]

    other = lax.ppermute(block, "req", route(lambda i: i ^ 1))
    two = jnp.where(core == 0, jnp.concatenate([block, other], 1), jnp.concatenate([other, block], 1))
    two = [two[0], two[1]]
    other = both(two, lambda i: i ^ 2)
    four = [
        jnp.where(pair == 0, jnp.concatenate([t, o], 0), jnp.concatenate([o, t], 0))
        for t, o in zip(two, other)
    ]
    walked = [four]
    for _ in range(reach):
        walked.append(both(walked[-1], lambda i: i + 4 if i % 2 == 0 else i - 4))
    early = [jnp.concatenate([w[kv] for w in walked[1 : reach - 1]], 0) for kv in range(2)]
    swapped = both(early, lambda i: i ^ 1)
    late = both(walked[reach - 1], lambda i: i ^ 1)
    return [[w[kv] for w in walked] + [swapped[kv], late[kv]] for kv in range(2)]


def attend_kernel(
    len_ref, group_ref, order_ref, owner_ref, q_ref, *refs,
    per_kv, half, n_blocks, n_pieces, n_dev, requests, tok_rows
):
    piece_refs = (refs[:n_pieces], refs[n_pieces : 2 * n_pieces])
    prev_ref, own_ref, o_ref, buf, sems = refs[2 * n_pieces :]
    h = pl.program_id(0)
    i = pl.program_id(1)
    r = lax.axis_index("req")
    base = r * tok_rows

    def span(k):
        length = len_ref[order_ref[k]]
        first = (k + 1) * tok_rows - length // 2
        return first, first + length

    k0 = jnp.maximum(r - 1, 0)
    k1 = jnp.minimum(r, requests - 1)
    start0, stop0 = span(k0)
    start1, stop1 = span(k1)
    start0 = jnp.where(r >= 1, start0, -1)
    stop0 = jnp.where(r >= 1, stop0, -1)
    start1 = jnp.where(r < requests, start1, -1)
    stop1 = jnp.where(r < requests, stop1, -1)
    start = jnp.where(h == 0, start0, start1)
    stop = jnp.where(h == 0, stop0, stop1)
    slot0 = base + h * half + i * TILE
    any_live = (start < slot0 + TILE) & (stop > slot0)
    rows = per_kv * TILE
    scale = 1.0 / math.sqrt(HD)
    block_rows = piece_refs[0][0].shape[1]
    group = piece_refs[0][0].shape[0]
    last = n_pieces - 1
    n_z = n_dev // 4
    reach = n_z // 2
    core = r % 2
    z = r // 4

    def position(hh, b):
        g = group_ref[order_ref[k0 if hh == 0 else k1]]
        d = owner_ref[g * n_blocks + b]
        o = (d // 4 - z + n_z) % n_z
        p0 = jnp.where(o == 0, 0, jnp.where(o >= reach, n_z - o, reach + o))
        p1 = jnp.where(o <= reach, o, reach + n_z - o)
        return jnp.where(core == 0, p0, p1) * 4 + d % 4

    def dst(hh, kv, b):
        return buf.at[hh, kv, pl.ds(b * block_rows, block_rows), :]

    def start_copy(hh, b):
        where = position(hh, b)
        place = where // group
        for p in range(n_pieces):
            if p <= reach:
                hit = place == p
                at = where % group
            elif p == reach + 1:
                hit = (place > reach) & (place < 2 * reach - 1)
                at = where - (reach + 1) * group
            else:
                hit = place == 2 * reach - 1
                at = where % group

            @pl.when(hit)
            def _():
                for kv in range(2):
                    pltpu.make_async_copy(
                        piece_refs[kv][p].at[at], dst(hh, kv, b), sems.at[hh, kv, b]
                    ).start()

    def wait_copy(hh, b):
        for kv in range(2):
            pltpu.make_async_copy(
                piece_refs[kv][0].at[0], dst(hh, kv, b), sems.at[hh, kv, b]
            ).wait()

    @pl.when((h == 0) & (i == 0))
    def _():
        for hh in range(2):
            for b in range(n_blocks):
                start_copy(hh, b)

    @pl.when(jnp.logical_not(any_live))
    def _():
        o_ref[...] = jnp.zeros_like(o_ref)

    def body(hh, chunks):
        @pl.when(i == 0)
        def _():
            for b in range(n_blocks):
                wait_copy(hh, b)

        @pl.when(any_live)
        def _():
            compute(hh, chunks)

    def compute(hh, chunks):
        kref = buf.at[hh, 0]
        vref = buf.at[hh, 1]
        q = jnp.concatenate([q_ref[:, j * HD : (j + 1) * HD] for j in range(per_kv)], axis=0)
        row = lax.broadcasted_iota(jnp.int32, (rows, 1), 0)
        slot = slot0 + jnp.bitwise_and(row, TILE - 1)
        live = (slot >= start) & (slot < stop)

        def raw(k):
            return lax.dot_general(
                q, k, (((1,), (1,)), ((), ())), preferred_element_type=jnp.float32
            )

        s_pre = raw(kref[...])
        m = jnp.max(s_pre, axis=1, keepdims=True) * scale
        suffix = []
        for kc, vc, key_base in chunks:
            key_slot = key_base + lax.broadcasted_iota(jnp.int32, (1, kc.shape[0]), 1)
            ok = (key_slot >= start) & (key_slot <= slot) & live
            s = raw(kc) * scale
            m = jnp.maximum(m, jnp.max(jnp.where(ok, s, masked_score), axis=1, keepdims=True))
            suffix.append((s, ok, vc))
        p = jnp.exp(s_pre * scale - m)
        l = jnp.sum(p, axis=1, keepdims=True)
        acc = jnp.dot(p.astype(jnp.bfloat16), vref[...], preferred_element_type=jnp.float32)
        for s, ok, vc in suffix:
            p = jnp.where(ok, jnp.exp(s - m), 0.0)
            l = l + jnp.sum(p, axis=1, keepdims=True)
            acc = acc + jnp.dot(p.astype(jnp.bfloat16), vc, preferred_element_type=jnp.float32)
        out = jnp.where(live, acc / jnp.where(live, l, 1.0), 0.0).astype(o_ref.dtype)
        for j in range(per_kv):
            o_ref[:, j * HD : (j + 1) * HD] = out[j * TILE : (j + 1) * TILE, :]

    skip = tok_rows - WINDOW

    @pl.when(h == 0)
    def _():
        body(
            0,
            [
                (prev_ref[0], prev_ref[1], base - WINDOW),
                (own_ref[0, :WINDOW], own_ref[1, :WINDOW], base),
            ],
        )

    @pl.when(h == 1)
    def _():
        body(1, [(own_ref[0, skip:], own_ref[1, skip:], base + skip)])


def per_device(
    queries, suffix_kv, prefix_kv, suffix_length, request_group, request_order, owner_map
):
    tok_rows = queries.shape[0]
    head_cols = suffix_kv.shape[2]
    per_kv = queries.shape[1] // head_cols
    stored_count = owner_map.shape[0]
    per_group = stored_count // GROUPS
    requests = suffix_length.shape[0]
    half = tok_rows // 2

    local = lax.all_to_all(prefix_kv, "tp", split_axis=3, concat_axis=2, tiled=True)
    pieces = ring_gather(local)
    earlier = from_behind(suffix_kv[:, tok_rows - WINDOW :, :], "req", 1)

    tiles_per_half = half // TILE
    grid = (2, tiles_per_half)
    n_pieces = len(pieces[0])
    kernel = functools.partial(
        attend_kernel,
        per_kv=per_kv,
        half=half,
        n_blocks=per_group,
        n_pieces=n_pieces,
        n_dev=lax.axis_size("req"),
        requests=requests,
        tok_rows=tok_rows,
    )
    block_rows = pieces[0][0].shape[1]
    prefix_rows = per_group * block_rows
    tile_map = lambda h, i, *s: (h * tiles_per_half + i, 0)
    whole = lambda h, i, *s: (0, 0, 0)
    return pl.pallas_call(
        kernel,
        out_shape=jax.ShapeDtypeStruct((tok_rows, per_kv * HD), queries.dtype),
        grid_spec=pltpu.PrefetchScalarGridSpec(
            num_scalar_prefetch=4,
            grid=grid,
            in_specs=[
                pl.BlockSpec((TILE, per_kv * HD), tile_map),
                *[pl.BlockSpec(memory_space=pl.ANY)] * (2 * n_pieces),
                pl.BlockSpec(earlier.shape, whole),
                pl.BlockSpec(suffix_kv.shape, whole),
            ],
            out_specs=pl.BlockSpec((TILE, per_kv * HD), tile_map),
            scratch_shapes=[
                pltpu.VMEM((2, 2, prefix_rows, HD), queries.dtype),
                pltpu.SemaphoreType.DMA((2, 2, per_group)),
            ],
        ),
        compiler_params=pltpu.CompilerParams(dimension_semantics=("arbitrary", "arbitrary")),
    )(
        suffix_length,
        request_group,
        request_order,
        owner_map,
        queries,
        *pieces[0],
        *pieces[1],
        earlier,
        suffix_kv,
    )


def solution(mesh):
    in_specs = (
        P("req", "tp"),
        P(None, "req", "tp"),
        P(None, "req", "tp", None),
        P(),
        P(),
        P(),
        P(),
    )
    out_specs = P("req", "tp")
    return jax.shard_map(
        per_device, mesh=mesh, in_specs=in_specs, out_specs=out_specs, check_vma=False
    )
```

```python
import functools
import math

import jax
import jax.numpy as jnp
from jax import lax
from jax.experimental import pallas as pl
from jax.experimental.pallas import tpu as pltpu
from jax.sharding import PartitionSpec as P

QH = 64
KVH = 8
HD = 128
GROUPS = 4

masked_score = -1e30
TILE = 96
WINDOW = 256


def from_behind(block, axis, distance):
    devices = range(lax.axis_size(axis))
    route = [(i - distance, i) for i in devices if i - distance in devices]
    return lax.ppermute(block, axis, route)


def ring_gather(block):
    n = lax.axis_size("req")
    r = lax.axis_index("req")
    core = r % 2
    pair = (r // 2) % 2
    reach = n // 8

    def route(fn):
        return [(i, fn(i) % n) for i in range(n)]

    def both(x, fn):
        return [lax.ppermute(x[kv], "req", route(fn)) for kv in range(2)]

    other = lax.ppermute(block, "req", route(lambda i: i ^ 1))
    two = jnp.where(core == 0, jnp.concatenate([block, other], 1), jnp.concatenate([other, block], 1))
    two = [two[0], two[1]]
    other = both(two, lambda i: i ^ 2)
    four = [
        jnp.where(pair == 0, jnp.concatenate([t, o], 0), jnp.concatenate([o, t], 0))
        for t, o in zip(two, other)
    ]
    walked = [four]
    for _ in range(reach):
        walked.append(both(walked[-1], lambda i: i + 4 if i % 2 == 0 else i - 4))
    mine = [jnp.concatenate([w[kv] for w in walked[1:reach]], 0) for kv in range(2)]
    swapped = both(mine, lambda i: i ^ 1)
    return [[w[kv] for w in walked] + [swapped[kv]] for kv in range(2)]


def attend_kernel(
    len_ref, group_ref, order_ref, owner_ref, q_ref, *refs,
    per_kv, half, n_blocks, n_pieces, n_dev, requests, tok_rows
):
    piece_refs = (refs[:n_pieces], refs[n_pieces : 2 * n_pieces])
    prev_ref, own_ref, o_ref, buf, sems = refs[2 * n_pieces :]
    h = pl.program_id(0)
    i = pl.program_id(1)
    r = lax.axis_index("req")
    base = r * tok_rows

    def span(k):
        length = len_ref[order_ref[k]]
        first = (k + 1) * tok_rows - length // 2
        return first, first + length

    k0 = jnp.maximum(r - 1, 0)
    k1 = jnp.minimum(r, requests - 1)
    start0, stop0 = span(k0)
    start1, stop1 = span(k1)
    start0 = jnp.where(r >= 1, start0, -1)
    stop0 = jnp.where(r >= 1, stop0, -1)
    start1 = jnp.where(r < requests, start1, -1)
    stop1 = jnp.where(r < requests, stop1, -1)
    start = jnp.where(h == 0, start0, start1)
    stop = jnp.where(h == 0, stop0, stop1)
    slot0 = base + h * half + i * TILE
    any_live = (start < slot0 + TILE) & (stop > slot0)
    rows = per_kv * TILE
    scale = 1.0 / math.sqrt(HD)
    block_rows = piece_refs[0][0].shape[1]
    group = piece_refs[0][0].shape[0]
    last = n_pieces - 1
    n_z = n_dev // 4
    reach = n_z // 2
    core = r % 2
    z = r // 4

    def position(hh, b):
        g = group_ref[order_ref[k0 if hh == 0 else k1]]
        d = owner_ref[g * n_blocks + b]
        o = (d // 4 - z + n_z) % n_z
        p0 = jnp.where(o == 0, 0, jnp.where(o >= reach, n_z - o, reach + o))
        p1 = jnp.where(o <= reach, o, reach + n_z - o)
        return jnp.where(core == 0, p0, p1) * 4 + d % 4

    def dst(hh, kv, b):
        return buf.at[hh, kv, pl.ds(b * block_rows, block_rows), :]

    def start_copy(hh, b):
        where = position(hh, b)
        place = where // group
        for p in range(n_pieces):
            hit = (place == p) if p < last else (place >= last)
            at = where % group if p < last else where - last * group

            @pl.when(hit)
            def _():
                for kv in range(2):
                    pltpu.make_async_copy(
                        piece_refs[kv][p].at[at], dst(hh, kv, b), sems.at[hh, kv, b]
                    ).start()

    def wait_copy(hh, b):
        for kv in range(2):
            pltpu.make_async_copy(
                piece_refs[kv][0].at[0], dst(hh, kv, b), sems.at[hh, kv, b]
            ).wait()

    @pl.when((h == 0) & (i == 0))
    def _():
        for hh in range(2):
            for b in range(n_blocks):
                start_copy(hh, b)

    @pl.when(jnp.logical_not(any_live))
    def _():
        o_ref[...] = jnp.zeros_like(o_ref)

    def body(hh, chunks):
        @pl.when(i == 0)
        def _():
            for b in range(n_blocks):
                wait_copy(hh, b)

        @pl.when(any_live)
        def _():
            compute(hh, chunks)

    def compute(hh, chunks):
        kref = buf.at[hh, 0]
        vref = buf.at[hh, 1]
        q = jnp.concatenate([q_ref[:, j * HD : (j + 1) * HD] for j in range(per_kv)], axis=0)
        row = lax.broadcasted_iota(jnp.int32, (rows, 1), 0)
        slot = slot0 + lax.rem(row, TILE)
        live = (slot >= start) & (slot < stop)

        def raw(k):
            return lax.dot_general(
                q, k, (((1,), (1,)), ((), ())), preferred_element_type=jnp.float32
            )

        s_pre = raw(kref[...])
        m = jnp.max(s_pre, axis=1, keepdims=True) * scale
        suffix = []
        for kc, vc, key_base in chunks:
            key_slot = key_base + lax.broadcasted_iota(jnp.int32, (1, kc.shape[0]), 1)
            ok = (key_slot >= start) & (key_slot <= slot) & live
            s = raw(kc) * scale
            m = jnp.maximum(m, jnp.max(jnp.where(ok, s, masked_score), axis=1, keepdims=True))
            suffix.append((s, ok, vc))
        p = jnp.exp(s_pre * scale - m)
        l = jnp.sum(p, axis=1, keepdims=True)
        acc = jnp.dot(p.astype(jnp.bfloat16), vref[...], preferred_element_type=jnp.float32)
        for s, ok, vc in suffix:
            p = jnp.where(ok, jnp.exp(s - m), 0.0)
            l = l + jnp.sum(p, axis=1, keepdims=True)
            acc = acc + jnp.dot(p.astype(jnp.bfloat16), vc, preferred_element_type=jnp.float32)
        out = jnp.where(live, acc / jnp.where(live, l, 1.0), 0.0).astype(o_ref.dtype)
        for j in range(per_kv):
            o_ref[:, j * HD : (j + 1) * HD] = out[j * TILE : (j + 1) * TILE, :]

    skip = tok_rows - WINDOW

    @pl.when(h == 0)
    def _():
        body(
            0,
            [
                (prev_ref[0], prev_ref[1], base - WINDOW),
                (own_ref[0, :WINDOW], own_ref[1, :WINDOW], base),
            ],
        )

    @pl.when(h == 1)
    def _():
        body(1, [(own_ref[0, skip:], own_ref[1, skip:], base + skip)])


def per_device(
    queries, suffix_kv, prefix_kv, suffix_length, request_group, request_order, owner_map
):
    tok_rows = queries.shape[0]
    head_cols = suffix_kv.shape[2]
    per_kv = queries.shape[1] // head_cols
    stored_count = owner_map.shape[0]
    per_group = stored_count // GROUPS
    requests = suffix_length.shape[0]
    half = tok_rows // 2

    local = lax.all_to_all(prefix_kv, "tp", split_axis=3, concat_axis=2, tiled=True)
    pieces = ring_gather(local)
    earlier = from_behind(suffix_kv[:, tok_rows - WINDOW :, :], "req", 1)

    tiles_per_half = half // TILE
    grid = (2, tiles_per_half)
    n_pieces = len(pieces[0])
    kernel = functools.partial(
        attend_kernel,
        per_kv=per_kv,
        half=half,
        n_blocks=per_group,
        n_pieces=n_pieces,
        n_dev=lax.axis_size("req"),
        requests=requests,
        tok_rows=tok_rows,
    )
    block_rows = pieces[0][0].shape[1]
    prefix_rows = per_group * block_rows
    tile_map = lambda h, i, *s: (h * tiles_per_half + i, 0)
    whole = lambda h, i, *s: (0, 0, 0)
    return pl.pallas_call(
        kernel,
        out_shape=jax.ShapeDtypeStruct((tok_rows, per_kv * HD), queries.dtype),
        grid_spec=pltpu.PrefetchScalarGridSpec(
            num_scalar_prefetch=4,
            grid=grid,
            in_specs=[
                pl.BlockSpec((TILE, per_kv * HD), tile_map),
                *[pl.BlockSpec(memory_space=pl.ANY)] * (2 * n_pieces),
                pl.BlockSpec(earlier.shape, whole),
                pl.BlockSpec(suffix_kv.shape, whole),
            ],
            out_specs=pl.BlockSpec((TILE, per_kv * HD), tile_map),
            scratch_shapes=[
                pltpu.VMEM((2, 2, prefix_rows, HD), queries.dtype),
                pltpu.SemaphoreType.DMA((2, 2, per_group)),
            ],
        ),
        compiler_params=pltpu.CompilerParams(dimension_semantics=("arbitrary", "arbitrary")),
    )(
        suffix_length,
        request_group,
        request_order,
        owner_map,
        queries,
        *pieces[0],
        *pieces[1],
        earlier,
        suffix_kv,
    )


def solution(mesh):
    in_specs = (
        P("req", "tp"),
        P(None, "req", "tp"),
        P(None, "req", "tp", None),
        P(),
        P(),
        P(),
        P(),
    )
    out_specs = P("req", "tp")
    return jax.shard_map(
        per_device, mesh=mesh, in_specs=in_specs, out_specs=out_specs, check_vma=False
    )
```
